512 devices in a mesh: ctx: 128 (over z, x, y_hi), tp: 4 (over y_lo, core).
Axes of the slice: x: 4, y: 8 (y_hi: 4, y_lo: 2; y = y_hi * 2 + y_lo), z: 8, core: 2. Of those that a mesh axis runs over, the one named last changes fastest.
Arguments:
- query_proj: bfloat16 [128, 131072], P('tp', 'ctx'), may hold values from -15 to 15
- key_proj: bfloat16 [128, 131072], P('tp', 'ctx'), may hold values from -6 to 6
- value_proj: bfloat16 [128, 131072], P('tp', 'ctx'), may hold values from -6 to 6
- short_taps: float32 [3, 128, 3], P(None, 'tp'), may hold values from -3 to 3
- long_filter: float32 [8, 131072], P('tp', 'ctx'), may hold values from -1.1 to 1.1, as said below
- skip_scale: float32 [128], P('tp'), may hold values from 0.5 to 1.5
- norm_gain: float32 [128], P('tp'), may hold values from 0.5 to 2
Outputs:
- mixer_out: bfloat16 [128, 131072], P('tp', 'ctx')
The draws below stay inside these ranges and needn't reach their ends.
Inputs may be any that keep to these rules, and one draw needn't show every extreme that they name: `long_filter`: filter taps.
All inputs are finite; a program needn't handle non-finite values.
Results may differ from the reference program's by a relative error of at most 0.001.
Values may be sent and summed in bfloat16 or wider, within the bound.
No kernel may reach another device: no remote copies, remote signals or barrier semaphores. Data moves between devices by JAX's collectives and lax.ppermute only.
A program may use at most 64 MiB of HBM per device.

```python
import math
import jax
import jax.numpy as jnp
from jax import lax

CH = 128
GROUP = 16
LEN = 131072
PADDED = 262144
FG = 8


def draw_query_proj(key, part):
    channel_scale = 0.5 * 6.0 ** (jnp.arange(CH, dtype=jnp.float32) / (CH - 1))
    base_draw = jnp.clip(jax.random.normal(key, (CH, LEN), jnp.float32), -5.0, 5.0)
    return (base_draw * channel_scale[:, None]).astype(jnp.bfloat16)


def draw_long_filter(key, part):
    key_rate, key_base = jax.random.split(key)
    positions = jnp.arange(LEN, dtype=jnp.float32)[None, :]
    log_decay = jax.random.uniform(key_rate, (FG, 1), jnp.float32, math.log(30.0), math.log(4.0 * LEN))
    base_draw = jnp.clip(jax.random.normal(key_base, (FG, LEN), jnp.float32), -5.0, 5.0)
    decay_len = jnp.exp(log_decay)
    norm_factor = jnp.sqrt(2.0 / (decay_len * -jnp.expm1(-2.0 * LEN / decay_len)))
    return base_draw * jnp.exp(-positions / decay_len) * norm_factor * 0.8


def levels(key, dims, cuts, smallest, top_value):
    def one(position, parts):
        heights = jax.random.uniform(jax.random.fold_in(jax.random.fold_in(key, 6), position), (parts,), jnp.float32, smallest / len(cuts), top_value / len(cuts))
        return jnp.repeat(jnp.exp(heights), dims[position] // parts).reshape((-1,) + (1,) * (len(dims) - position - 1))

    factor_of = one(*cuts[0])
    for cut in cuts[1:]:
        factor_of = factor_of * one(*cut)
    return factor_of


def normal_values(rng, shape, deviation, bound, cuts=(), kind=jnp.bfloat16):
    result = jax.random.normal(rng, shape, jnp.float32) * deviation
    if len(cuts) > 0:
        result = levels(rng, shape, cuts, -0.22, 0.18) * result
    return jnp.clip(result, min=-bound, max=bound).astype(kind)


def setup_inputs(seed: int = 0) -> dict:
    keys = jax.random.split(jax.random.key(seed), 8)
    query_proj = draw_query_proj(jax.random.fold_in(keys[7], 71), 0)
    key_proj = normal_values(keys[1], (CH, LEN), 1.0, 6.0, ((0, 4), (1, 128)))
    value_proj = normal_values(keys[2], (CH, LEN), 1.0, 6.0, ((0, 4), (1, 128)))
    short_taps = normal_values(keys[3], (3, CH, 3), 0.6, 3.0, ((1, 4),), jnp.float32)
    long_filter = draw_long_filter(jax.random.fold_in(keys[7], 71), 0)
    skip_scale = jnp.clip(0.5 + 1.0 * jax.random.uniform(keys[5], (CH,), jnp.float32) ** levels(keys[5], (CH,), ((0, 4),), -0.2, 0.2), 0.5, 1.5)
    norm_gain = jnp.clip(jnp.exp(math.log(2.0) - 1.3862944 * jax.random.uniform(keys[6], (CH,), jnp.float32) ** levels(keys[6], (CH,), ((0, 4),), -0.2, 0.2)), 0.5, 2.0)
    return dict(query_proj=query_proj, key_proj=key_proj, value_proj=value_proj, short_taps=short_taps, long_filter=long_filter, skip_scale=skip_scale, norm_gain=norm_gain)


def short_conv(values, taps):
    padded = jnp.pad(values.astype(jnp.float32), ((0, 0), (2, 0)))
    return taps[:, 0:1] * padded[:, 2:] + taps[:, 1:2] * padded[:, 1:-1] + taps[:, 2:3] * padded[:, :-2]

def reference(query_proj, key_proj, value_proj, short_taps, long_filter, skip_scale, norm_gain):
    q_conv = short_conv(query_proj, short_taps[0])
    k_conv = short_conv(key_proj, short_taps[1])
    v_conv = short_conv(value_proj, short_taps[2])
    product = k_conv * v_conv
    grouped = product.reshape(FG, GROUP, LEN)

    def one_group(group_pair):
        inputs, filt_row = group_pair
        spectrum = jnp.fft.rfft(inputs, n=PADDED, axis=-1) * jnp.fft.rfft(filt_row, n=PADDED)[None, :]
        return jnp.fft.irfft(spectrum, n=PADDED, axis=-1)[:, :LEN]
    convolved = lax.map(one_group, (grouped, long_filter)).reshape(CH, LEN)
    mixed = q_conv * (convolved + skip_scale[:, None] * product)
    power = lax.optimization_barrier(jnp.mean(mixed * mixed, axis=0))
    return (norm_gain[:, None] * mixed * lax.rsqrt(power + 1e-05)).astype(jnp.bfloat16)
```

```python
import math

import jax
import jax.numpy as jnp
from jax import lax
from jax.sharding import PartitionSpec as P

HIGHEST = lax.Precision.HIGHEST


def shifted(x, axis, by):
    length = lax.axis_size(axis)
    pairs = [(i, i + by) for i in range(length) if 0 <= i + by < length]
    return lax.ppermute(x, axis, pairs)


def trig_pair(steps_int, modulus):
    angle = (steps_int % modulus).astype(jnp.float32) * (2.0 * math.pi / modulus)
    return (jnp.cos(angle), jnp.sin(angle))


def grid_product(first_len, second_len, modulus):
    left = lax.broadcasted_iota(jnp.int32, (first_len, second_len), 0)
    right = lax.broadcasted_iota(jnp.int32, (first_len, second_len), 1)
    return trig_pair(left * right, modulus)


def apply_rows(table, values):
    return jnp.einsum("kt,ctn->ckn", table, values, precision=HIGHEST)


def apply_cols(table, values):
    return jnp.einsum("ckn,nm->ckm", values, table, precision=HIGHEST)


def dft_section(apply_fn, real_part, imag_part, tables, direction):
    cos_table, sin_table = tables
    if imag_part is None:
        return (apply_fn(cos_table, real_part), direction * apply_fn(sin_table, real_part))
    new_real = apply_fn(cos_table, real_part) - direction * apply_fn(sin_table, imag_part)
    new_imag = direction * apply_fn(sin_table, real_part) + apply_fn(cos_table, imag_part)
    return (new_real, new_imag)


def rotate(real_part, imag_part, tables, direction):
    cos_table, sin_table = tables
    new_real = real_part * cos_table - direction * imag_part * sin_table
    new_imag = direction * real_part * sin_table + imag_part * cos_table
    return (new_real, new_imag)


def forward_local(real_part, imag_part, first_len, ctx_count, ctx_index):
    rows_real = real_part.shape[1]
    padded_len = first_len * ctx_count * ctx_count
    extra_rows = ((0, 0), (0, first_len - rows_real), (0, 0))
    real_part = jnp.pad(real_part, extra_rows)
    imag_part = jnp.pad(imag_part, extra_rows)
    first_tables = grid_product(first_len, first_len, first_len)
    real_part, imag_part = dft_section(apply_rows, real_part, imag_part, first_tables, -1.0)
    real_part, imag_part = rotate(
        real_part, imag_part, grid_product(first_len, ctx_count, first_len * ctx_count), -1.0
    )
    real_part, imag_part = dft_section(
        apply_cols, real_part, imag_part, grid_product(ctx_count, ctx_count, ctx_count), -1.0
    )
    freq_first = lax.broadcasted_iota(jnp.int32, (first_len, ctx_count), 0)
    freq_second = lax.broadcasted_iota(jnp.int32, (first_len, ctx_count), 1)
    twist = trig_pair((freq_first + first_len * freq_second) * ctx_index, padded_len)
    return rotate(real_part, imag_part, twist, -1.0)


def causal_three(values, before, taps):
    extended = jnp.concatenate([before.astype(jnp.float32), values.astype(jnp.float32)], axis=1)
    return (
        taps[:, 0:1] * extended[:, 2:]
        + taps[:, 1:2] * extended[:, 1:-1]
        + taps[:, 2:3] * extended[:, :-2]
    )


def pack_pairs(values, filter_count):
    grouped = values.reshape((filter_count, 2, -1) + values.shape[1:])
    return (
        grouped[:, 0].reshape((-1,) + values.shape[1:]),
        grouped[:, 1].reshape((-1,) + values.shape[1:]),
    )


def unpack_pairs(real_part, imag_part, filter_count):
    shape = (filter_count, 1, -1) + real_part.shape[1:]
    both = jnp.concatenate([real_part.reshape(shape), imag_part.reshape(shape)], axis=1)
    return both.reshape((-1,) + real_part.shape[1:])


def shards(query_proj, key_proj, value_proj, short_taps, long_filter, skip_scale, norm_gain):
    chan_count = query_proj.shape[0]
    tok_count = query_proj.shape[1]
    ctx_count = lax.axis_size("ctx")
    ctx_index = lax.axis_index("ctx")
    row_count = tok_count // ctx_count
    first_len = 2 * row_count
    padded_len = first_len * ctx_count * ctx_count
    filter_count = long_filter.shape[0]
    pair_count = chan_count // 2
    tails = jnp.stack([query_proj[:, -2:], key_proj[:, -2:], value_proj[:, -2:]])
    before = shifted(tails, "ctx", 1)
    q_conv = causal_three(query_proj, before[0], short_taps[0])
    k_conv = causal_three(key_proj, before[1], short_taps[1])
    v_conv = causal_three(value_proj, before[2], short_taps[2])
    product = k_conv * v_conv
    both_in = jnp.concatenate(
        [
            product.reshape(chan_count, row_count, ctx_count),
            long_filter.reshape(filter_count, row_count, ctx_count),
        ],
        axis=0,
    )
    moved = lax.all_to_all(both_in, "ctx", split_axis=2, concat_axis=1, tiled=True)
    moved = moved.reshape(chan_count + filter_count, row_count, ctx_count)
    data_cols = moved[:chan_count]
    filter_cols = moved[chan_count:]
    pair_real, pair_imag = pack_pairs(data_cols, filter_count)
    in_real = jnp.concatenate([pair_real, filter_cols], axis=0)
    in_imag = jnp.concatenate([pair_imag, jnp.zeros_like(filter_cols)], axis=0)
    spec_real, spec_imag = forward_local(in_real, in_imag, first_len, ctx_count, ctx_index)
    spec = lax.all_to_all(
        jnp.concatenate([spec_real, spec_imag], axis=0), "ctx", split_axis=2, concat_axis=2,
        tiled=True,
    )
    square_tables = grid_product(ctx_count, ctx_count, ctx_count)
    row_total = pair_count + filter_count
    spec_real, spec_imag = dft_section(
        apply_cols, spec[:row_total], spec[row_total:], square_tables, -1.0
    )
    data_real = spec_real[:pair_count]
    data_imag = spec_imag[:pair_count]
    filt_real = spec_real[pair_count:]
    filt_imag = spec_imag[pair_count:]
    grouped_shape = (filter_count, pair_count // filter_count, first_len, ctx_count)
    group_real = data_real.reshape(grouped_shape)
    group_imag = data_imag.reshape(grouped_shape)
    prod_real = (group_real * filt_real[:, None] - group_imag * filt_imag[:, None]).reshape(
        data_real.shape
    )
    prod_imag = (group_real * filt_imag[:, None] + group_imag * filt_real[:, None]).reshape(
        data_real.shape
    )
    back_real, back_imag = dft_section(apply_cols, prod_real, prod_imag, square_tables, 1.0)
    freq_first = lax.broadcasted_iota(jnp.int32, (first_len, ctx_count), 0)
    time_third = lax.broadcasted_iota(jnp.int32, (first_len, ctx_count), 1)
    twist = trig_pair((freq_first + first_len * ctx_index) * time_third, padded_len)
    back_real, back_imag = rotate(back_real, back_imag, twist, 1.0)
    back = lax.all_to_all(
        jnp.concatenate([back_real, back_imag], axis=0), "ctx", split_axis=2, concat_axis=2,
        tiled=True,
    )
    back_real, back_imag = dft_section(
        apply_cols, back[:pair_count], back[pair_count:], square_tables, 1.0
    )
    back_real, back_imag = rotate(
        back_real, back_imag, grid_product(first_len, ctx_count, first_len * ctx_count), 1.0
    )
    first_tables = grid_product(first_len, first_len, first_len)
    time_real, time_imag = dft_section(apply_rows, back_real, back_imag, first_tables, 1.0)
    time_vals = unpack_pairs(time_real[:, :row_count], time_imag[:, :row_count], filter_count)
    time_vals = time_vals.reshape(chan_count, row_count * ctx_count, 1) * (1.0 / padded_len)
    convolved = lax.all_to_all(time_vals, "ctx", split_axis=1, concat_axis=2, tiled=True).reshape(
        chan_count, tok_count
    )
    mixed = q_conv * (convolved + skip_scale[:, None] * product)
    power = lax.psum(jnp.sum(mixed * mixed, axis=0), "tp")
    total_channels = chan_count * lax.axis_size("tp")
    return (norm_gain[:, None] * mixed * lax.rsqrt(power / total_channels + 1e-05)).astype(
        jnp.bfloat16
    )


def solution(mesh):
    return jax.shard_map(
        shards,
        mesh=mesh,
        in_specs=(
            P("tp", "ctx"),
            P("tp", "ctx"),
            P("tp", "ctx"),
            P(None, "tp", None),
            P("tp", "ctx"),
            P("tp"),
            P("tp"),
        ),
        out_specs=P("tp", "ctx"),
        check_vma=False,
    )
```

```python
import math

import jax
import jax.numpy as jnp
from jax import lax
from jax.sharding import PartitionSpec as P

HIGHEST = lax.Precision.HIGHEST


def shifted(x, axis, by):
    length = lax.axis_size(axis)
    pairs = [(i, i + by) for i in range(length) if 0 <= i + by < length]
    return lax.ppermute(x, axis, pairs)


def trig_pair(steps_int, modulus):
    angle = (steps_int % modulus).astype(jnp.float32) * (2.0 * math.pi / modulus)
    return (jnp.cos(angle), jnp.sin(angle))


def grid_product(first_len, second_len, modulus):
    left = lax.broadcasted_iota(jnp.int32, (first_len, second_len), 0)
    right = lax.broadcasted_iota(jnp.int32, (first_len, second_len), 1)
    return trig_pair(left * right, modulus)


def apply_rows(table, values):
    return jnp.einsum("kt,ctn->ckn", table, values, precision=HIGHEST)


def apply_cols(table, values):
    return jnp.einsum("ckn,nm->ckm", values, table, precision=HIGHEST)


def dft_section(apply_fn, real_part, imag_part, tables, direction):
    cos_table, sin_table = tables
    if imag_part is None:
        return (apply_fn(cos_table, real_part), direction * apply_fn(sin_table, real_part))
    new_real = apply_fn(cos_table, real_part) - direction * apply_fn(sin_table, imag_part)
    new_imag = direction * apply_fn(sin_table, real_part) + apply_fn(cos_table, imag_part)
    return (new_real, new_imag)


def rotate(real_part, imag_part, tables, direction):
    cos_table, sin_table = tables
    new_real = real_part * cos_table - direction * imag_part * sin_table
    new_imag = direction * real_part * sin_table + imag_part * cos_table
    return (new_real, new_imag)


def forward_local(real_part, imag_part, first_len, ctx_count, ctx_index):
    rows_real = real_part.shape[1]
    padded_len = first_len * ctx_count * ctx_count
    extra_rows = ((0, 0), (0, first_len - rows_real), (0, 0))
    real_part = jnp.pad(real_part, extra_rows)
    imag_part = jnp.pad(imag_part, extra_rows)
    first_tables = grid_product(first_len, first_len, first_len)
    real_part, imag_part = dft_section(apply_rows, real_part, imag_part, first_tables, -1.0)
    real_part, imag_part = rotate(
        real_part, imag_part, grid_product(first_len, ctx_count, first_len * ctx_count), -1.0
    )
    real_part, imag_part = dft_section(
        apply_cols, real_part, imag_part, grid_product(ctx_count, ctx_count, ctx_count), -1.0
    )
    freq_first = lax.broadcasted_iota(jnp.int32, (first_len, ctx_count), 0)
    freq_second = lax.broadcasted_iota(jnp.int32, (first_len, ctx_count), 1)
    twist = trig_pair((freq_first + first_len * freq_second) * ctx_index, padded_len)
    return rotate(real_part, imag_part, twist, -1.0)


def causal_three(values, before, taps):
    extended = jnp.concatenate([before.astype(jnp.float32), values.astype(jnp.float32)], axis=1)
    return (
        taps[:, 0:1] * extended[:, 2:]
        + taps[:, 1:2] * extended[:, 1:-1]
        + taps[:, 2:3] * extended[:, :-2]
    )


def exchange_sum(x, axis):
    length = lax.axis_size(axis)
    step = 1
    while step < length:
        x = x + lax.ppermute(x, axis, [(i, i ^ step) for i in range(length)])
        step *= 2
    return x


def pack_pairs(values, filter_count):
    grouped = values.reshape((filter_count, 2, -1) + values.shape[1:])
    return (
        grouped[:, 0].reshape((-1,) + values.shape[1:]),
        grouped[:, 1].reshape((-1,) + values.shape[1:]),
    )


def unpack_pairs(real_part, imag_part, filter_count):
    shape = (filter_count, 1, -1) + real_part.shape[1:]
    both = jnp.concatenate([real_part.reshape(shape), imag_part.reshape(shape)], axis=1)
    return both.reshape((-1,) + real_part.shape[1:])


def shards(query_proj, key_proj, value_proj, short_taps, long_filter, skip_scale, norm_gain):
    chan_count = query_proj.shape[0]
    tok_count = query_proj.shape[1]
    ctx_count = lax.axis_size("ctx")
    ctx_index = lax.axis_index("ctx")
    row_count = tok_count // ctx_count
    first_len = 2 * row_count
    padded_len = first_len * ctx_count * ctx_count
    filter_count = long_filter.shape[0]
    pair_count = chan_count // 2
    tails = jnp.stack([query_proj[:, -2:], key_proj[:, -2:], value_proj[:, -2:]])
    before = shifted(tails, "ctx", 1)
    q_conv = causal_three(query_proj, before[0], short_taps[0])
    k_conv = causal_three(key_proj, before[1], short_taps[1])
    v_conv = causal_three(value_proj, before[2], short_taps[2])
    product = k_conv * v_conv
    both_in = jnp.concatenate(
        [
            product.reshape(chan_count, row_count, ctx_count),
            long_filter.reshape(filter_count, row_count, ctx_count),
        ],
        axis=0,
    )
    moved = lax.all_to_all(both_in, "ctx", split_axis=2, concat_axis=1, tiled=True)
    moved = moved.reshape(chan_count + filter_count, row_count, ctx_count)
    data_cols = moved[:chan_count]
    filter_cols = moved[chan_count:]
    pair_real, pair_imag = pack_pairs(data_cols, filter_count)
    in_real = jnp.concatenate([pair_real, filter_cols], axis=0)
    in_imag = jnp.concatenate([pair_imag, jnp.zeros_like(filter_cols)], axis=0)
    spec_real, spec_imag = forward_local(in_real, in_imag, first_len, ctx_count, ctx_index)
    spec = lax.all_to_all(
        jnp.concatenate([spec_real, spec_imag], axis=0), "ctx", split_axis=2, concat_axis=2,
        tiled=True,
    )
    square_tables = grid_product(ctx_count, ctx_count, ctx_count)
    row_total = pair_count + filter_count
    spec_real, spec_imag = dft_section(
        apply_cols, spec[:row_total], spec[row_total:], square_tables, -1.0
    )
    data_real = spec_real[:pair_count]
    data_imag = spec_imag[:pair_count]
    filt_real = spec_real[pair_count:]
    filt_imag = spec_imag[pair_count:]
    grouped_shape = (filter_count, pair_count // filter_count, first_len, ctx_count)
    group_real = data_real.reshape(grouped_shape)
    group_imag = data_imag.reshape(grouped_shape)
    prod_real = (group_real * filt_real[:, None] - group_imag * filt_imag[:, None]).reshape(
        data_real.shape
    )
    prod_imag = (group_real * filt_imag[:, None] + group_imag * filt_real[:, None]).reshape(
        data_real.shape
    )
    back_real, back_imag = dft_section(apply_cols, prod_real, prod_imag, square_tables, 1.0)
    freq_first = lax.broadcasted_iota(jnp.int32, (first_len, ctx_count), 0)
    time_third = lax.broadcasted_iota(jnp.int32, (first_len, ctx_count), 1)
    twist = trig_pair((freq_first + first_len * ctx_index) * time_third, padded_len)
    back_real, back_imag = rotate(back_real, back_imag, twist, 1.0)
    back = lax.all_to_all(
        jnp.concatenate([back_real, back_imag], axis=0), "ctx", split_axis=2, concat_axis=2,
        tiled=True,
    )
    back_real, back_imag = dft_section(
        apply_cols, back[:pair_count], back[pair_count:], square_tables, 1.0
    )
    back_real, back_imag = rotate(
        back_real, back_imag, grid_product(first_len, ctx_count, first_len * ctx_count), 1.0
    )
    first_tables = grid_product(first_len, first_len, first_len)
    time_real, time_imag = dft_section(apply_rows, back_real, back_imag, first_tables, 1.0)
    time_vals = unpack_pairs(time_real[:, :row_count], time_imag[:, :row_count], filter_count)
    time_vals = time_vals.reshape(chan_count, row_count * ctx_count, 1) * (1.0 / padded_len)
    convolved = lax.all_to_all(time_vals, "ctx", split_axis=1, concat_axis=2, tiled=True).reshape(
        chan_count, tok_count
    )
    mixed = q_conv * (convolved + skip_scale[:, None] * product)
    power = exchange_sum(jnp.sum(mixed * mixed, axis=0), "tp")
    total_channels = chan_count * lax.axis_size("tp")
    return (norm_gain[:, None] * mixed * lax.rsqrt(power / total_channels + 1e-05)).astype(
        jnp.bfloat16
    )


def solution(mesh):
    return jax.shard_map(
        shards,
        mesh=mesh,
        in_specs=(
            P("tp", "ctx"),
            P("tp", "ctx"),
            P("tp", "ctx"),
            P(None, "tp", None),
            P("tp", "ctx"),
            P("tp"),
            P("tp"),
        ),
        out_specs=P("tp", "ctx"),
        check_vma=False,
    )
```

```python
import math

import jax
import jax.numpy as jnp
from jax import lax
from jax.sharding import PartitionSpec as P

HIGHEST = lax.Precision.HIGHEST


def shifted(x, axis, by):
    length = lax.axis_size(axis)
    pairs = [(i, i + by) for i in range(length) if 0 <= i + by < length]
    return lax.ppermute(x, axis, pairs)


def trig_pair(steps_int, modulus):
    angle = (steps_int % modulus).astype(jnp.float32) * (2.0 * math.pi / modulus)
    return (jnp.cos(angle), jnp.sin(angle))


def grid_product(first_len, second_len, modulus):
    left = lax.broadcasted_iota(jnp.int32, (first_len, second_len), 0)
    right = lax.broadcasted_iota(jnp.int32, (first_len, second_len), 1)
    return trig_pair(left * right, modulus)


def apply_rows(table, values):
    return jnp.einsum("kt,ctn->ckn", table, values, precision=HIGHEST)


def apply_cols(table, values):
    return jnp.einsum("ckn,nm->ckm", values, table, precision=HIGHEST)


def dft_section(apply_fn, real_part, imag_part, tables, direction):
    cos_table, sin_table = tables
    if imag_part is None:
        return (apply_fn(cos_table, real_part), direction * apply_fn(sin_table, real_part))
    new_real = apply_fn(cos_table, real_part) - direction * apply_fn(sin_table, imag_part)
    new_imag = direction * apply_fn(sin_table, real_part) + apply_fn(cos_table, imag_part)
    return (new_real, new_imag)


def rotate(real_part, imag_part, tables, direction):
    cos_table, sin_table = tables
    new_real = real_part * cos_table - direction * imag_part * sin_table
    new_imag = direction * real_part * sin_table + imag_part * cos_table
    return (new_real, new_imag)


def forward_local(real_part, imag_part, first_len, ctx_count, ctx_index):
    rows_real = real_part.shape[1]
    padded_len = first_len * ctx_count * ctx_count
    first_tables = grid_product(first_len, rows_real, first_len)
    real_part, imag_part = dft_section(apply_rows, real_part, imag_part, first_tables, -1.0)
    real_part, imag_part = rotate(
        real_part, imag_part, grid_product(first_len, ctx_count, first_len * ctx_count), -1.0
    )
    real_part, imag_part = dft_section(
        apply_cols, real_part, imag_part, grid_product(ctx_count, ctx_count, ctx_count), -1.0
    )
    freq_first = lax.broadcasted_iota(jnp.int32, (first_len, ctx_count), 0)
    freq_second = lax.broadcasted_iota(jnp.int32, (first_len, ctx_count), 1)
    twist = trig_pair((freq_first + first_len * freq_second) * ctx_index, padded_len)
    return rotate(real_part, imag_part, twist, -1.0)


def causal_three(values, before, taps):
    extended = jnp.concatenate([before.astype(jnp.float32), values.astype(jnp.float32)], axis=1)
    return (
        taps[:, 0:1] * extended[:, 2:]
        + taps[:, 1:2] * extended[:, 1:-1]
        + taps[:, 2:3] * extended[:, :-2]
    )


def shards(query_proj, key_proj, value_proj, short_taps, long_filter, skip_scale, norm_gain):
    chan_count = query_proj.shape[0]
    tok_count = query_proj.shape[1]
    ctx_count = lax.axis_size("ctx")
    ctx_index = lax.axis_index("ctx")
    row_count = tok_count // ctx_count
    first_len = 2 * row_count
    padded_len = first_len * ctx_count * ctx_count
    filter_count = long_filter.shape[0]
    pair_count = chan_count // 2
    tails = jnp.stack([query_proj[:, -2:], key_proj[:, -2:], value_proj[:, -2:]])
    before = shifted(tails, "ctx", 1)
    q_conv = causal_three(query_proj, before[0], short_taps[0])
    k_conv = causal_three(key_proj, before[1], short_taps[1])
    v_conv = causal_three(value_proj, before[2], short_taps[2])
    product = k_conv * v_conv
    halves = product.reshape(filter_count, 2, -1, tok_count)
    both_in = jnp.concatenate(
        [
            halves[:, 0].reshape(pair_count, tok_count),
            long_filter,
            halves[:, 1].reshape(pair_count, tok_count),
            jnp.zeros_like(long_filter),
        ],
        axis=0,
    )
    row_total = pair_count + filter_count
    moved = lax.all_to_all(
        both_in.reshape(2 * row_total, row_count, ctx_count), "ctx", split_axis=2, concat_axis=1,
        tiled=True,
    )
    moved = moved.reshape(2 * row_total, row_count, ctx_count)
    spec_real, spec_imag = forward_local(
        moved[:row_total], moved[row_total:], first_len, ctx_count, ctx_index
    )
    spec = lax.all_to_all(
        jnp.concatenate([spec_real, spec_imag], axis=0), "ctx", split_axis=2, concat_axis=2,
        tiled=True,
    )
    square_tables = grid_product(ctx_count, ctx_count, ctx_count)
    spec_real, spec_imag = dft_section(
        apply_cols, spec[:row_total], spec[row_total:], square_tables, -1.0
    )
    data_real = spec_real[:pair_count]
    data_imag = spec_imag[:pair_count]
    filt_real = spec_real[pair_count:]
    filt_imag = spec_imag[pair_count:]
    grouped_shape = (filter_count, pair_count // filter_count, first_len, ctx_count)
    group_real = data_real.reshape(grouped_shape)
    group_imag = data_imag.reshape(grouped_shape)
    prod_real = (group_real * filt_real[:, None] - group_imag * filt_imag[:, None]).reshape(
        data_real.shape
    )
    prod_imag = (group_real * filt_imag[:, None] + group_imag * filt_real[:, None]).reshape(
        data_real.shape
    )
    back_real, back_imag = dft_section(apply_cols, prod_real, prod_imag, square_tables, 1.0)
    freq_first = lax.broadcasted_iota(jnp.int32, (first_len, ctx_count), 0)
    time_third = lax.broadcasted_iota(jnp.int32, (first_len, ctx_count), 1)
    twist = trig_pair((freq_first + first_len * ctx_index) * time_third, padded_len)
    back_real, back_imag = rotate(back_real, back_imag, twist, 1.0)
    back = lax.all_to_all(
        jnp.concatenate([back_real, back_imag], axis=0), "ctx", split_axis=2, concat_axis=2,
        tiled=True,
    )
    back_real, back_imag = dft_section(
        apply_cols, back[:pair_count], back[pair_count:], square_tables, 1.0
    )
    back_real, back_imag = rotate(
        back_real, back_imag, grid_product(first_len, ctx_count, first_len * ctx_count), 1.0
    )
    last_tables = grid_product(row_count, first_len, first_len)
    time_real, time_imag = dft_section(apply_rows, back_real, back_imag, last_tables, 1.0)
    time_vals = jnp.concatenate([time_real, time_imag], axis=0)
    time_vals = time_vals.reshape(chan_count, row_count * ctx_count, 1) * (1.0 / padded_len)
    convolved = lax.all_to_all(time_vals, "ctx", split_axis=1, concat_axis=2, tiled=True)
    convolved = convolved.reshape(2, filter_count, -1, tok_count).transpose(1, 0, 2, 3)
    convolved = convolved.reshape(chan_count, tok_count)
    mixed = q_conv * (convolved + skip_scale[:, None] * product)
    power = lax.psum(jnp.sum(mixed * mixed, axis=0), "tp")
    total_channels = chan_count * lax.axis_size("tp")
    return (norm_gain[:, None] * mixed * lax.rsqrt(power / total_channels + 1e-05)).astype(
        jnp.bfloat16
    )


def solution(mesh):
    return jax.shard_map(
        shards,
        mesh=mesh,
        in_specs=(
            P("tp", "ctx"),
            P("tp", "ctx"),
            P("tp", "ctx"),
            P(None, "tp", None),
            P("tp", "ctx"),
            P("tp"),
            P("tp"),
        ),
        out_specs=P("tp", "ctx"),
        check_vma=False,
    )
```

```python
import math

import jax
import jax.numpy as jnp
from jax import lax
from jax.experimental import pallas as pl
from jax.experimental.pallas import tpu as pltpu
from jax.sharding import PartitionSpec as P

INTERPRET = False

HIGHEST = lax.Precision.HIGHEST


def shifted(x, axis, by):
    length = lax.axis_size(axis)
    pairs = [(i, i + by) for i in range(length) if 0 <= i + by < length]
    return lax.ppermute(x, axis, pairs)


def trig_pair(steps_int, modulus):
    angle = (steps_int % modulus).astype(jnp.float32) * (2.0 * math.pi / modulus)
    return (jnp.cos(angle), jnp.sin(angle))


def grid_product(first_len, second_len, modulus):
    left = lax.broadcasted_iota(jnp.int32, (first_len, second_len), 0)
    right = lax.broadcasted_iota(jnp.int32, (first_len, second_len), 1)
    return trig_pair(left * right, modulus)


def apply_rows(table, values):
    return jnp.einsum("kt,ctn->ckn", table, values, precision=HIGHEST)


def apply_cols(table, values):
    return jnp.einsum("ckn,nm->ckm", values, table, precision=HIGHEST)


def dft_section(apply_fn, real_part, imag_part, tables, direction):
    cos_table, sin_table = tables
    if imag_part is None:
        return (apply_fn(cos_table, real_part), direction * apply_fn(sin_table, real_part))
    new_real = apply_fn(cos_table, real_part) - direction * apply_fn(sin_table, imag_part)
    new_imag = direction * apply_fn(sin_table, real_part) + apply_fn(cos_table, imag_part)
    return (new_real, new_imag)


def rotate(real_part, imag_part, tables, direction):
    cos_table, sin_table = tables
    new_real = real_part * cos_table - direction * imag_part * sin_table
    new_imag = direction * real_part * sin_table + imag_part * cos_table
    return (new_real, new_imag)


def forward_local(real_part, imag_part, first_len, ctx_count, ctx_index):
    rows_real = real_part.shape[1]
    padded_len = first_len * ctx_count * ctx_count
    first_tables = grid_product(first_len, rows_real, first_len)
    real_part, imag_part = dft_section(apply_rows, real_part, imag_part, first_tables, -1.0)
    real_part, imag_part = rotate(
        real_part, imag_part, grid_product(first_len, ctx_count, first_len * ctx_count), -1.0
    )
    real_part, imag_part = dft_section(
        apply_cols, real_part, imag_part, grid_product(ctx_count, ctx_count, ctx_count), -1.0
    )
    freq_first = lax.broadcasted_iota(jnp.int32, (first_len, ctx_count), 0)
    freq_second = lax.broadcasted_iota(jnp.int32, (first_len, ctx_count), 1)
    twist = trig_pair((freq_first + first_len * freq_second) * ctx_index, padded_len)
    return rotate(real_part, imag_part, twist, -1.0)


def causal_three(values, before, taps):
    extended = jnp.concatenate([before.astype(jnp.float32), values.astype(jnp.float32)], axis=1)
    return (
        taps[:, 0:1] * extended[:, 2:]
        + taps[:, 1:2] * extended[:, 1:-1]
        + taps[:, 2:3] * extended[:, :-2]
    )


def spectral_kernel(spec_ref, cos_ref, sin_ref, twc_ref, tws_ref, out_ref):
    filter_count = (spec_ref.shape[0] - out_ref.shape[0]) // 2
    pair_count = out_ref.shape[0] // 2
    first_len, ctx_count = spec_ref.shape[1], spec_ref.shape[2]
    row_total = pair_count + filter_count
    cos_t = cos_ref[...]
    sin_t = sin_ref[...]

    def dot(a, b):
        return jnp.dot(a, b, precision=HIGHEST, preferred_element_type=jnp.float32)

    flat = (pair_count * first_len, ctx_count)
    filt_flat = (filter_count * first_len, ctx_count)
    x_re = spec_ref[0:pair_count].reshape(flat)
    x_im = spec_ref[row_total : row_total + pair_count].reshape(flat)
    h_re = spec_ref[pair_count:row_total].reshape(filt_flat)
    h_im = spec_ref[row_total + pair_count :].reshape(filt_flat)
    y_re = dot(x_re, cos_t) + dot(x_im, sin_t)
    y_im = dot(x_im, cos_t) - dot(x_re, sin_t)
    g_re = dot(h_re, cos_t) + dot(h_im, sin_t)
    g_im = dot(h_im, cos_t) - dot(h_re, sin_t)
    grouped = (filter_count, pair_count // filter_count, first_len, ctx_count)
    y_re = y_re.reshape(grouped)
    y_im = y_im.reshape(grouped)
    g_re = g_re.reshape(filter_count, 1, first_len, ctx_count)
    g_im = g_im.reshape(filter_count, 1, first_len, ctx_count)
    p_re = (y_re * g_re - y_im * g_im).reshape(flat)
    p_im = (y_re * g_im + y_im * g_re).reshape(flat)
    b_re = (dot(p_re, cos_t) - dot(p_im, sin_t)).reshape(pair_count, first_len, ctx_count)
    b_im = (dot(p_re, sin_t) + dot(p_im, cos_t)).reshape(pair_count, first_len, ctx_count)
    tw_c = twc_ref[...][None]
    tw_s = tws_ref[...][None]
    out_ref[0:pair_count] = b_re * tw_c - b_im * tw_s
    out_ref[pair_count:] = b_re * tw_s + b_im * tw_c


def shards(query_proj, key_proj, value_proj, short_taps, long_filter, skip_scale, norm_gain):
    chan_count = query_proj.shape[0]
    tok_count = query_proj.shape[1]
    ctx_count = lax.axis_size("ctx")
    ctx_index = lax.axis_index("ctx")
    row_count = tok_count // ctx_count
    first_len = 2 * row_count
    padded_len = first_len * ctx_count * ctx_count
    filter_count = long_filter.shape[0]
    pair_count = chan_count // 2
    tails = jnp.stack([query_proj[:, -2:], key_proj[:, -2:], value_proj[:, -2:]])
    before = shifted(tails, "ctx", 1)
    q_conv = causal_three(query_proj, before[0], short_taps[0])
    k_conv = causal_three(key_proj, before[1], short_taps[1])
    v_conv = causal_three(value_proj, before[2], short_taps[2])
    product = k_conv * v_conv
    halves = product.reshape(filter_count, 2, -1, tok_count)
    both_in = jnp.concatenate(
        [
            halves[:, 0].reshape(pair_count, tok_count),
            long_filter,
            halves[:, 1].reshape(pair_count, tok_count),
            jnp.zeros_like(long_filter),
        ],
        axis=0,
    )
    row_total = pair_count + filter_count
    moved = lax.all_to_all(
        both_in.reshape(2 * row_total, row_count, ctx_count), "ctx", split_axis=2, concat_axis=1,
        tiled=True,
    )
    moved = moved.reshape(2 * row_total, row_count, ctx_count)
    spec_real, spec_imag = forward_local(
        moved[:row_total], moved[row_total:], first_len, ctx_count, ctx_index
    )
    spec = lax.all_to_all(
        jnp.concatenate([spec_real, spec_imag], axis=0), "ctx", split_axis=2, concat_axis=2,
        tiled=True,
    )
    square_tables = grid_product(ctx_count, ctx_count, ctx_count)
    freq_first = lax.broadcasted_iota(jnp.int32, (first_len, ctx_count), 0)
    time_third = lax.broadcasted_iota(jnp.int32, (first_len, ctx_count), 1)
    twist = trig_pair((freq_first + first_len * ctx_index) * time_third, padded_len)
    back_both = pl.pallas_call(
        spectral_kernel,
        out_shape=jax.ShapeDtypeStruct((2 * pair_count, first_len, ctx_count), jnp.float32),
        interpret=INTERPRET,
    )(spec, square_tables[0], square_tables[1], twist[0], twist[1])
    back = lax.all_to_all(
        back_both, "ctx", split_axis=2, concat_axis=2,
        tiled=True,
    )
    back_real, back_imag = dft_section(
        apply_cols, back[:pair_count], back[pair_count:], square_tables, 1.0
    )
    back_real, back_imag = rotate(
        back_real, back_imag, grid_product(first_len, ctx_count, first_len * ctx_count), 1.0
    )
    last_tables = grid_product(row_count, first_len, first_len)
    time_real, time_imag = dft_section(apply_rows, back_real, back_imag, last_tables, 1.0)
    time_vals = jnp.concatenate([time_real, time_imag], axis=0)
    time_vals = time_vals.reshape(chan_count, row_count * ctx_count, 1) * (1.0 / padded_len)
    convolved = lax.all_to_all(time_vals, "ctx", split_axis=1, concat_axis=2, tiled=True)
    convolved = convolved.reshape(2, filter_count, -1, tok_count).transpose(1, 0, 2, 3)
    convolved = convolved.reshape(chan_count, tok_count)
    mixed = q_conv * (convolved + skip_scale[:, None] * product)
    power = lax.psum(jnp.sum(mixed * mixed, axis=0), "tp")
    total_channels = chan_count * lax.axis_size("tp")
    return (norm_gain[:, None] * mixed * lax.rsqrt(power / total_channels + 1e-05)).astype(
        jnp.bfloat16
    )


def solution(mesh):
    return jax.shard_map(
        shards,
        mesh=mesh,
        in_specs=(
            P("tp", "ctx"),
            P("tp", "ctx"),
            P("tp", "ctx"),
            P(None, "tp", None),
            P("tp", "ctx"),
            P("tp"),
            P("tp"),
        ),
        out_specs=P("tp", "ctx"),
        check_vma=False,
    )
```

```python
import math

import jax
import jax.numpy as jnp
from jax import lax
from jax.sharding import PartitionSpec as P

HIGHEST = lax.Precision.HIGHEST


def shifted(x, axis, by):
    length = lax.axis_size(axis)
    pairs = [(i, i + by) for i in range(length) if 0 <= i + by < length]
    return lax.ppermute(x, axis, pairs)


def trig_pair(steps_int, modulus):
    angle = (steps_int % modulus).astype(jnp.float32) * (2.0 * math.pi / modulus)
    return (jnp.cos(angle), jnp.sin(angle))


def grid_product(first_len, second_len, modulus):
    left = lax.broadcasted_iota(jnp.int32, (first_len, second_len), 0)
    right = lax.broadcasted_iota(jnp.int32, (first_len, second_len), 1)
    return trig_pair(left * right, modulus)


def apply_rows(table, values):
    return jnp.einsum("kt,ctn->ckn", table, values, precision=HIGHEST)


def apply_cols(table, values):
    return jnp.einsum("ckn,nm->ckm", values, table, precision=HIGHEST)


def dft_section(apply_fn, real_part, imag_part, tables, direction):
    cos_table, sin_table = tables
    if imag_part is None:
        return (apply_fn(cos_table, real_part), direction * apply_fn(sin_table, real_part))
    new_real = apply_fn(cos_table, real_part) - direction * apply_fn(sin_table, imag_part)
    new_imag = direction * apply_fn(sin_table, real_part) + apply_fn(cos_table, imag_part)
    return (new_real, new_imag)


def rotate(real_part, imag_part, tables, direction):
    cos_table, sin_table = tables
    new_real = real_part * cos_table - direction * imag_part * sin_table
    new_imag = direction * real_part * sin_table + imag_part * cos_table
    return (new_real, new_imag)


def forward_local(real_part, imag_part, first_len, ctx_count, ctx_index):
    rows_real = real_part.shape[1]
    padded_len = first_len * ctx_count * ctx_count
    first_tables = grid_product(first_len, rows_real, first_len)
    real_part, imag_part = dft_section(apply_rows, real_part, imag_part, first_tables, -1.0)
    real_part, imag_part = rotate(
        real_part, imag_part, grid_product(first_len, ctx_count, first_len * ctx_count), -1.0
    )
    real_part, imag_part = dft_section(
        apply_cols, real_part, imag_part, grid_product(ctx_count, ctx_count, ctx_count), -1.0
    )
    freq_first = lax.broadcasted_iota(jnp.int32, (first_len, ctx_count), 0)
    freq_second = lax.broadcasted_iota(jnp.int32, (first_len, ctx_count), 1)
    twist = trig_pair((freq_first + first_len * freq_second) * ctx_index, padded_len)
    return rotate(real_part, imag_part, twist, -1.0)


def causal_three(values, before, taps):
    extended = jnp.concatenate([before.astype(jnp.float32), values.astype(jnp.float32)], axis=1)
    return (
        taps[:, 0:1] * extended[:, 2:]
        + taps[:, 1:2] * extended[:, 1:-1]
        + taps[:, 2:3] * extended[:, :-2]
    )


def row_blocks(tables, direction):
    cos_table, sin_table = tables
    return jnp.stack(
        [
            jnp.stack([cos_table, -direction * sin_table], axis=1),
            jnp.stack([direction * sin_table, cos_table], axis=1),
        ]
    )


def col_blocks(tables, direction):
    cos_table, sin_table = tables
    return jnp.stack(
        [
            jnp.stack([cos_table, direction * sin_table], axis=1),
            jnp.stack([-direction * sin_table, cos_table], axis=1),
        ]
    )


def complex_rows(tables, values, direction):
    return jnp.einsum("ukst,ctsn->ckun", row_blocks(tables, direction), values, precision=HIGHEST)


def complex_cols(tables, values, direction):
    return jnp.einsum("cksn,snum->ckum", values, col_blocks(tables, direction), precision=HIGHEST)


def complex_rotate(values, tables, direction):
    cos_table, sin_table = tables
    real_part = values[:, :, 0]
    imag_part = values[:, :, 1]
    new_real = real_part * cos_table - direction * imag_part * sin_table
    new_imag = direction * real_part * sin_table + imag_part * cos_table
    return jnp.stack([new_real, new_imag], axis=2)


def shards(query_proj, key_proj, value_proj, short_taps, long_filter, skip_scale, norm_gain):
    chan_count = query_proj.shape[0]
    tok_count = query_proj.shape[1]
    ctx_count = lax.axis_size("ctx")
    ctx_index = lax.axis_index("ctx")
    row_count = tok_count // ctx_count
    first_len = 2 * row_count
    padded_len = first_len * ctx_count * ctx_count
    filter_count = long_filter.shape[0]
    pair_count = chan_count // 2
    tails = jnp.stack([query_proj[:, -2:], key_proj[:, -2:], value_proj[:, -2:]])
    before = shifted(tails, "ctx", 1)
    q_conv = causal_three(query_proj, before[0], short_taps[0])
    k_conv = causal_three(key_proj, before[1], short_taps[1])
    v_conv = causal_three(value_proj, before[2], short_taps[2])
    product = k_conv * v_conv
    halves = product.reshape(filter_count, 2, -1, tok_count)
    both_in = jnp.concatenate(
        [
            halves[:, 0].reshape(pair_count, tok_count),
            long_filter,
            halves[:, 1].reshape(pair_count, tok_count),
            jnp.zeros_like(long_filter),
        ],
        axis=0,
    )
    row_total = pair_count + filter_count
    moved = lax.all_to_all(
        both_in.reshape(2 * row_total, row_count, ctx_count), "ctx", split_axis=2, concat_axis=1,
        tiled=True,
    )
    values = moved.reshape(2, row_total, row_count, ctx_count).transpose(1, 2, 0, 3)
    values = complex_rows(grid_product(first_len, row_count, first_len), values, -1.0)
    values = complex_rotate(
        values, grid_product(first_len, ctx_count, first_len * ctx_count), -1.0
    )
    square_tables = grid_product(ctx_count, ctx_count, ctx_count)
    values = complex_cols(square_tables, values, -1.0)
    freq_first = lax.broadcasted_iota(jnp.int32, (first_len, ctx_count), 0)
    freq_second = lax.broadcasted_iota(jnp.int32, (first_len, ctx_count), 1)
    twist = trig_pair((freq_first + first_len * freq_second) * ctx_index, padded_len)
    values = complex_rotate(values, twist, -1.0)
    spec = lax.all_to_all(values, "ctx", split_axis=3, concat_axis=3, tiled=True)
    spec = complex_cols(square_tables, spec, -1.0)
    data = spec[:pair_count].reshape(filter_count, pair_count // filter_count, first_len, 2, ctx_count)
    filt = spec[pair_count:][:, None]
    prod_real = data[:, :, :, 0] * filt[:, :, :, 0] - data[:, :, :, 1] * filt[:, :, :, 1]
    prod_imag = data[:, :, :, 0] * filt[:, :, :, 1] + data[:, :, :, 1] * filt[:, :, :, 0]
    prod = jnp.stack([prod_real, prod_imag], axis=3).reshape(pair_count, first_len, 2, ctx_count)
    back = complex_cols(square_tables, prod, 1.0)
    time_third = lax.broadcasted_iota(jnp.int32, (first_len, ctx_count), 1)
    twist = trig_pair((freq_first + first_len * ctx_index) * time_third, padded_len)
    back = complex_rotate(back, twist, 1.0)
    back = lax.all_to_all(back, "ctx", split_axis=3, concat_axis=3, tiled=True)
    back = complex_cols(square_tables, back, 1.0)
    back = complex_rotate(
        back, grid_product(first_len, ctx_count, first_len * ctx_count), 1.0
    )
    time_vals = complex_rows(grid_product(row_count, first_len, first_len), back, 1.0)
    time_vals = time_vals.transpose(2, 0, 1, 3)
    time_vals = time_vals.reshape(chan_count, row_count * ctx_count, 1) * (1.0 / padded_len)
    convolved = lax.all_to_all(time_vals, "ctx", split_axis=1, concat_axis=2, tiled=True)
    convolved = convolved.reshape(2, filter_count, -1, tok_count).transpose(1, 0, 2, 3)
    convolved = convolved.reshape(chan_count, tok_count)
    mixed = q_conv * (convolved + skip_scale[:, None] * product)
    power = lax.psum(jnp.sum(mixed * mixed, axis=0), "tp")
    total_channels = chan_count * lax.axis_size("tp")
    return (norm_gain[:, None] * mixed * lax.rsqrt(power / total_channels + 1e-05)).astype(
        jnp.bfloat16
    )


def solution(mesh):
    return jax.shard_map(
        shards,
        mesh=mesh,
        in_specs=(
            P("tp", "ctx"),
            P("tp", "ctx"),
            P("tp", "ctx"),
            P(None, "tp", None),
            P("tp", "ctx"),
            P("tp"),
            P("tp"),
        ),
        out_specs=P("tp", "ctx"),
        check_vma=False,
    )
```

```python
import math

import jax
import jax.numpy as jnp
from jax import lax
from jax.sharding import PartitionSpec as P

HIGHEST = lax.Precision.HIGHEST


def shifted(x, axis, by):
    length = lax.axis_size(axis)
    pairs = [(i, i + by) for i in range(length) if 0 <= i + by < length]
    return lax.ppermute(x, axis, pairs)


def trig_pair(steps_int, modulus):
    angle = (steps_int % modulus).astype(jnp.float32) * (2.0 * math.pi / modulus)
    return (jnp.cos(angle), jnp.sin(angle))


def grid_product(first_len, second_len, modulus):
    left = lax.broadcasted_iota(jnp.int32, (first_len, second_len), 0)
    right = lax.broadcasted_iota(jnp.int32, (first_len, second_len), 1)
    return trig_pair(left * right, modulus)


def apply_rows(table, values):
    return jnp.einsum("kt,ctn->ckn", table, values, precision=HIGHEST)


def apply_cols(table, values):
    return jnp.einsum("ckn,nm->ckm", values, table, precision=HIGHEST)


def dft_section(apply_fn, real_part, imag_part, tables, direction):
    cos_table, sin_table = tables
    if imag_part is None:
        return (apply_fn(cos_table, real_part), direction * apply_fn(sin_table, real_part))
    if apply_fn is apply_cols:
        block = jnp.concatenate(
            [
                jnp.concatenate([cos_table, direction * sin_table], axis=1),
                jnp.concatenate([-direction * sin_table, cos_table], axis=1),
            ],
            axis=0,
        )
        both = apply_cols(block, jnp.concatenate([real_part, imag_part], axis=2))
        out_len = cos_table.shape[1]
        return (both[:, :, :out_len], both[:, :, out_len:])
    block = jnp.concatenate(
        [
            jnp.concatenate([cos_table, -direction * sin_table], axis=1),
            jnp.concatenate([direction * sin_table, cos_table], axis=1),
        ],
        axis=0,
    )
    both = apply_rows(block, jnp.concatenate([real_part, imag_part], axis=1))
    out_len = cos_table.shape[0]
    return (both[:, :out_len], both[:, out_len:])


def rotate(real_part, imag_part, tables, direction):
    cos_table, sin_table = tables
    new_real = real_part * cos_table - direction * imag_part * sin_table
    new_imag = direction * real_part * sin_table + imag_part * cos_table
    return (new_real, new_imag)


def forward_local(real_part, imag_part, first_len, ctx_count, ctx_index):
    rows_real = real_part.shape[1]
    padded_len = first_len * ctx_count * ctx_count
    first_tables = grid_product(first_len, rows_real, first_len)
    real_part, imag_part = dft_section(apply_rows, real_part, imag_part, first_tables, -1.0)
    real_part, imag_part = rotate(
        real_part, imag_part, grid_product(first_len, ctx_count, first_len * ctx_count), -1.0
    )
    real_part, imag_part = dft_section(
        apply_cols, real_part, imag_part, grid_product(ctx_count, ctx_count, ctx_count), -1.0
    )
    freq_first = lax.broadcasted_iota(jnp.int32, (first_len, ctx_count), 0)
    freq_second = lax.broadcasted_iota(jnp.int32, (first_len, ctx_count), 1)
    twist = trig_pair((freq_first + first_len * freq_second) * ctx_index, padded_len)
    return rotate(real_part, imag_part, twist, -1.0)


def causal_three(values, before, taps):
    extended = jnp.concatenate([before.astype(jnp.float32), values.astype(jnp.float32)], axis=1)
    return (
        taps[:, 0:1] * extended[:, 2:]
        + taps[:, 1:2] * extended[:, 1:-1]
        + taps[:, 2:3] * extended[:, :-2]
    )


def shards(query_proj, key_proj, value_proj, short_taps, long_filter, skip_scale, norm_gain):
    chan_count = query_proj.shape[0]
    tok_count = query_proj.shape[1]
    ctx_count = lax.axis_size("ctx")
    ctx_index = lax.axis_index("ctx")
    row_count = tok_count // ctx_count
    first_len = 2 * row_count
    padded_len = first_len * ctx_count * ctx_count
    filter_count = long_filter.shape[0]
    pair_count = chan_count // 2
    tails = jnp.stack([query_proj[:, -2:], key_proj[:, -2:], value_proj[:, -2:]])
    before = shifted(tails, "ctx", 1)
    q_conv = causal_three(query_proj, before[0], short_taps[0])
    k_conv = causal_three(key_proj, before[1], short_taps[1])
    v_conv = causal_three(value_proj, before[2], short_taps[2])
    product = k_conv * v_conv
    halves = product.reshape(filter_count, 2, -1, tok_count)
    both_in = jnp.concatenate(
        [
            halves[:, 0].reshape(pair_count, tok_count),
            long_filter,
            halves[:, 1].reshape(pair_count, tok_count),
            jnp.zeros_like(long_filter),
        ],
        axis=0,
    )
    row_total = pair_count + filter_count
    moved = lax.all_to_all(
        both_in.reshape(2 * row_total, row_count, ctx_count), "ctx", split_axis=2, concat_axis=1,
        tiled=True,
    )
    moved = moved.reshape(2 * row_total, row_count, ctx_count)
    spec_real, spec_imag = forward_local(
        moved[:row_total], moved[row_total:], first_len, ctx_count, ctx_index
    )
    spec = lax.all_to_all(
        jnp.concatenate([spec_real, spec_imag], axis=0), "ctx", split_axis=2, concat_axis=2,
        tiled=True,
    )
    square_tables = grid_product(ctx_count, ctx_count, ctx_count)
    spec_real, spec_imag = dft_section(
        apply_cols, spec[:row_total], spec[row_total:], square_tables, -1.0
    )
    data_real = spec_real[:pair_count]
    data_imag = spec_imag[:pair_count]
    filt_real = spec_real[pair_count:]
    filt_imag = spec_imag[pair_count:]
    grouped_shape = (filter_count, pair_count // filter_count, first_len, ctx_count)
    group_real = data_real.reshape(grouped_shape)
    group_imag = data_imag.reshape(grouped_shape)
    prod_real = (group_real * filt_real[:, None] - group_imag * filt_imag[:, None]).reshape(
        data_real.shape
    )
    prod_imag = (group_real * filt_imag[:, None] + group_imag * filt_real[:, None]).reshape(
        data_real.shape
    )
    back_real, back_imag = dft_section(apply_cols, prod_real, prod_imag, square_tables, 1.0)
    freq_first = lax.broadcasted_iota(jnp.int32, (first_len, ctx_count), 0)
    time_third = lax.broadcasted_iota(jnp.int32, (first_len, ctx_count), 1)
    twist = trig_pair((freq_first + first_len * ctx_index) * time_third, padded_len)
    back_real, back_imag = rotate(back_real, back_imag, twist, 1.0)
    back = lax.all_to_all(
        jnp.concatenate([back_real, back_imag], axis=0), "ctx", split_axis=2, concat_axis=2,
        tiled=True,
    )
    back_real, back_imag = dft_section(
        apply_cols, back[:pair_count], back[pair_count:], square_tables, 1.0
    )
    back_real, back_imag = rotate(
        back_real, back_imag, grid_product(first_len, ctx_count, first_len * ctx_count), 1.0
    )
    last_tables = grid_product(row_count, first_len, first_len)
    time_real, time_imag = dft_section(apply_rows, back_real, back_imag, last_tables, 1.0)
    time_vals = jnp.concatenate([time_real, time_imag], axis=0)
    time_vals = time_vals.reshape(chan_count, row_count * ctx_count, 1) * (1.0 / padded_len)
    convolved = lax.all_to_all(time_vals, "ctx", split_axis=1, concat_axis=2, tiled=True)
    convolved = convolved.reshape(2, filter_count, -1, tok_count).transpose(1, 0, 2, 3)
    convolved = convolved.reshape(chan_count, tok_count)
    mixed = q_conv * (convolved + skip_scale[:, None] * product)
    power = lax.psum(jnp.sum(mixed * mixed, axis=0), "tp")
    total_channels = chan_count * lax.axis_size("tp")
    return (norm_gain[:, None] * mixed * lax.rsqrt(power / total_channels + 1e-05)).astype(
        jnp.bfloat16
    )


def solution(mesh):
    return jax.shard_map(
        shards,
        mesh=mesh,
        in_specs=(
            P("tp", "ctx"),
            P("tp", "ctx"),
            P("tp", "ctx"),
            P(None, "tp", None),
            P("tp", "ctx"),
            P("tp"),
            P("tp"),
        ),
        out_specs=P("tp", "ctx"),
        check_vma=False,
    )
```

```python
import math

import jax
import jax.numpy as jnp
from jax import lax
from jax.sharding import PartitionSpec as P

HIGHEST = lax.Precision.HIGHEST


def shifted(x, axis, by):
    length = lax.axis_size(axis)
    pairs = [(i, i + by) for i in range(length) if 0 <= i + by < length]
    return lax.ppermute(x, axis, pairs)


def trig_pair(steps_int, modulus):
    angle = (steps_int % modulus).astype(jnp.float32) * (2.0 * math.pi / modulus)
    return (jnp.cos(angle), jnp.sin(angle))


def grid_product(first_len, second_len, modulus):
    left = lax.broadcasted_iota(jnp.int32, (first_len, second_len), 0)
    right = lax.broadcasted_iota(jnp.int32, (first_len, second_len), 1)
    return trig_pair(left * right, modulus)


def apply_rows(table, values):
    return jnp.einsum("kt,ctn->ckn", table, values, precision=HIGHEST)


def apply_cols(table, values):
    return jnp.einsum("ckn,nm->ckm", values, table, precision=HIGHEST)


def dft_section(apply_fn, real_part, imag_part, tables, direction):
    cos_table, sin_table = tables
    if imag_part is None:
        return (apply_fn(cos_table, real_part), direction * apply_fn(sin_table, real_part))
    if apply_fn is apply_cols:
        block = jnp.concatenate(
            [
                jnp.concatenate([cos_table, direction * sin_table], axis=1),
                jnp.concatenate([-direction * sin_table, cos_table], axis=1),
            ],
            axis=0,
        )
        both = apply_cols(block, jnp.concatenate([real_part, imag_part], axis=2))
        out_len = cos_table.shape[1]
        return (both[:, :, :out_len], both[:, :, out_len:])
    block = jnp.concatenate(
        [
            jnp.concatenate([cos_table, -direction * sin_table], axis=1),
            jnp.concatenate([direction * sin_table, cos_table], axis=1),
        ],
        axis=0,
    )
    both = apply_rows(block, jnp.concatenate([real_part, imag_part], axis=1))
    out_len = cos_table.shape[0]
    return (both[:, :out_len], both[:, out_len:])


def rotate(real_part, imag_part, tables, direction):
    cos_table, sin_table = tables
    new_real = real_part * cos_table - direction * imag_part * sin_table
    new_imag = direction * real_part * sin_table + imag_part * cos_table
    return (new_real, new_imag)


def forward_local(real_part, imag_part, first_len, ctx_count, ctx_index):
    rows_real = real_part.shape[1]
    padded_len = first_len * ctx_count * ctx_count
    first_tables = grid_product(first_len, rows_real, first_len)
    real_part, imag_part = dft_section(apply_rows, real_part, imag_part, first_tables, -1.0)
    real_part, imag_part = rotate(
        real_part, imag_part, grid_product(first_len, ctx_count, first_len * ctx_count), -1.0
    )
    real_part, imag_part = dft_section(
        apply_cols, real_part, imag_part, grid_product(ctx_count, ctx_count, ctx_count), -1.0
    )
    freq_first = lax.broadcasted_iota(jnp.int32, (first_len, ctx_count), 0)
    freq_second = lax.broadcasted_iota(jnp.int32, (first_len, ctx_count), 1)
    twist = trig_pair((freq_first + first_len * freq_second) * ctx_index, padded_len)
    return rotate(real_part, imag_part, twist, -1.0)


def causal_three(values, before, taps):
    extended = jnp.concatenate([before.astype(jnp.float32), values.astype(jnp.float32)], axis=1)
    return (
        taps[:, 0:1] * extended[:, 2:]
        + taps[:, 1:2] * extended[:, 1:-1]
        + taps[:, 2:3] * extended[:, :-2]
    )


def shards(query_proj, key_proj, value_proj, short_taps, long_filter, skip_scale, norm_gain):
    chan_count = query_proj.shape[0]
    tok_count = query_proj.shape[1]
    ctx_count = lax.axis_size("ctx")
    ctx_index = lax.axis_index("ctx")
    row_count = tok_count // ctx_count
    first_len = 2 * row_count
    padded_len = first_len * ctx_count * ctx_count
    filter_count = long_filter.shape[0]
    pair_count = chan_count // 2
    tile = min(128, tok_count)
    tails = jnp.stack([query_proj[:, -tile:], key_proj[:, -tile:], value_proj[:, -tile:]])
    before = shifted(tails, "ctx", 1)[:, :, -2:]
    q_conv = causal_three(query_proj, before[0], short_taps[0])
    k_conv = causal_three(key_proj, before[1], short_taps[1])
    v_conv = causal_three(value_proj, before[2], short_taps[2])
    product = k_conv * v_conv
    halves = product.reshape(filter_count, 2, -1, tok_count)
    both_in = jnp.concatenate(
        [
            halves[:, 0].reshape(pair_count, tok_count),
            long_filter,
            halves[:, 1].reshape(pair_count, tok_count),
            jnp.zeros_like(long_filter),
        ],
        axis=0,
    )
    row_total = pair_count + filter_count
    moved = lax.all_to_all(
        both_in.reshape(2 * row_total, row_count, ctx_count), "ctx", split_axis=2, concat_axis=1,
        tiled=True,
    )
    moved = moved.reshape(2 * row_total, row_count, ctx_count)
    spec_real, spec_imag = forward_local(
        moved[:row_total], moved[row_total:], first_len, ctx_count, ctx_index
    )
    spec = lax.all_to_all(
        jnp.concatenate([spec_real, spec_imag], axis=0), "ctx", split_axis=2, concat_axis=2,
        tiled=True,
    )
    square_tables = grid_product(ctx_count, ctx_count, ctx_count)
    spec_real, spec_imag = dft_section(
        apply_cols, spec[:row_total], spec[row_total:], square_tables, -1.0
    )
    data_real = spec_real[:pair_count]
    data_imag = spec_imag[:pair_count]
    filt_real = spec_real[pair_count:]
    filt_imag = spec_imag[pair_count:]
    grouped_shape = (filter_count, pair_count // filter_count, first_len, ctx_count)
    group_real = data_real.reshape(grouped_shape)
    group_imag = data_imag.reshape(grouped_shape)
    prod_real = (group_real * filt_real[:, None] - group_imag * filt_imag[:, None]).reshape(
        data_real.shape
    )
    prod_imag = (group_real * filt_imag[:, None] + group_imag * filt_real[:, None]).reshape(
        data_real.shape
    )
    back_real, back_imag = dft_section(apply_cols, prod_real, prod_imag, square_tables, 1.0)
    freq_first = lax.broadcasted_iota(jnp.int32, (first_len, ctx_count), 0)
    time_third = lax.broadcasted_iota(jnp.int32, (first_len, ctx_count), 1)
    twist = trig_pair((freq_first + first_len * ctx_index) * time_third, padded_len)
    back_real, back_imag = rotate(back_real, back_imag, twist, 1.0)
    back = lax.all_to_all(
        jnp.concatenate([back_real, back_imag], axis=0), "ctx", split_axis=2, concat_axis=2,
        tiled=True,
    )
    back_real, back_imag = dft_section(
        apply_cols, back[:pair_count], back[pair_count:], square_tables, 1.0
    )
    back_real, back_imag = rotate(
        back_real, back_imag, grid_product(first_len, ctx_count, first_len * ctx_count), 1.0
    )
    last_tables = grid_product(row_count, first_len, first_len)
    time_real, time_imag = dft_section(apply_rows, back_real, back_imag, last_tables, 1.0)
    time_vals = jnp.concatenate([time_real, time_imag], axis=0)
    time_vals = time_vals.reshape(chan_count, row_count * ctx_count, 1) * (1.0 / padded_len)
    convolved = lax.all_to_all(time_vals, "ctx", split_axis=1, concat_axis=2, tiled=True)
    convolved = convolved.reshape(2, filter_count, -1, tok_count).transpose(1, 0, 2, 3)
    convolved = convolved.reshape(chan_count, tok_count)
    mixed = q_conv * (convolved + skip_scale[:, None] * product)
    power = lax.psum(jnp.sum(mixed * mixed, axis=0), "tp")
    total_channels = chan_count * lax.axis_size("tp")
    return (norm_gain[:, None] * mixed * lax.rsqrt(power / total_channels + 1e-05)).astype(
        jnp.bfloat16
    )


def solution(mesh):
    return jax.shard_map(
        shards,
        mesh=mesh,
        in_specs=(
            P("tp", "ctx"),
            P("tp", "ctx"),
            P("tp", "ctx"),
            P(None, "tp", None),
            P("tp", "ctx"),
            P("tp"),
            P("tp"),
        ),
        out_specs=P("tp", "ctx"),
        check_vma=False,
    )
```

```python
import math

import jax
import jax.numpy as jnp
from jax import lax
from jax.sharding import PartitionSpec as P

MATMUL_PRECISION = lax.Precision.HIGH


def shifted(x, axis, by):
    length = lax.axis_size(axis)
    pairs = [(i, i + by) for i in range(length) if 0 <= i + by < length]
    return lax.ppermute(x, axis, pairs)


def trig_pair(steps_int, modulus):
    angle = (steps_int % modulus).astype(jnp.float32) * (2.0 * math.pi / modulus)
    return (jnp.cos(angle), jnp.sin(angle))


def grid_product(first_len, second_len, modulus):
    left = lax.broadcasted_iota(jnp.int32, (first_len, second_len), 0)
    right = lax.broadcasted_iota(jnp.int32, (first_len, second_len), 1)
    return trig_pair(left * right, modulus)


def apply_rows(table, values):
    return jnp.einsum("kt,ctn->ckn", table, values, precision=MATMUL_PRECISION)


def apply_cols(table, values):
    return jnp.einsum("ckn,nm->ckm", values, table, precision=MATMUL_PRECISION)


def dft_section(apply_fn, real_part, imag_part, tables, direction):
    cos_table, sin_table = tables
    if imag_part is None:
        return (apply_fn(cos_table, real_part), direction * apply_fn(sin_table, real_part))
    if apply_fn is apply_cols:
        block = jnp.concatenate(
            [
                jnp.concatenate([cos_table, direction * sin_table], axis=1),
                jnp.concatenate([-direction * sin_table, cos_table], axis=1),
            ],
            axis=0,
        )
        both = apply_cols(block, jnp.concatenate([real_part, imag_part], axis=2))
        out_len = cos_table.shape[1]
        return (both[:, :, :out_len], both[:, :, out_len:])
    block = jnp.concatenate(
        [
            jnp.concatenate([cos_table, -direction * sin_table], axis=1),
            jnp.concatenate([direction * sin_table, cos_table], axis=1),
        ],
        axis=0,
    )
    both = apply_rows(block, jnp.concatenate([real_part, imag_part], axis=1))
    out_len = cos_table.shape[0]
    return (both[:, :out_len], both[:, out_len:])


def rotate(real_part, imag_part, tables, direction):
    cos_table, sin_table = tables
    new_real = real_part * cos_table - direction * imag_part * sin_table
    new_imag = direction * real_part * sin_table + imag_part * cos_table
    return (new_real, new_imag)


def forward_local(real_part, imag_part, first_len, ctx_count, ctx_index):
    rows_real = real_part.shape[1]
    padded_len = first_len * ctx_count * ctx_count
    first_tables = grid_product(first_len, rows_real, first_len)
    real_part, imag_part = dft_section(apply_rows, real_part, imag_part, first_tables, -1.0)
    real_part, imag_part = rotate(
        real_part, imag_part, grid_product(first_len, ctx_count, first_len * ctx_count), -1.0
    )
    real_part, imag_part = dft_section(
        apply_cols, real_part, imag_part, grid_product(ctx_count, ctx_count, ctx_count), -1.0
    )
    freq_first = lax.broadcasted_iota(jnp.int32, (first_len, ctx_count), 0)
    freq_second = lax.broadcasted_iota(jnp.int32, (first_len, ctx_count), 1)
    twist = trig_pair((freq_first + first_len * freq_second) * ctx_index, padded_len)
    return rotate(real_part, imag_part, twist, -1.0)


def causal_three(values, before, taps):
    extended = jnp.concatenate([before.astype(jnp.float32), values.astype(jnp.float32)], axis=1)
    return (
        taps[:, 0:1] * extended[:, 2:]
        + taps[:, 1:2] * extended[:, 1:-1]
        + taps[:, 2:3] * extended[:, :-2]
    )


def shards(query_proj, key_proj, value_proj, short_taps, long_filter, skip_scale, norm_gain):
    chan_count = query_proj.shape[0]
    tok_count = query_proj.shape[1]
    ctx_count = lax.axis_size("ctx")
    ctx_index = lax.axis_index("ctx")
    row_count = tok_count // ctx_count
    first_len = 2 * row_count
    padded_len = first_len * ctx_count * ctx_count
    filter_count = long_filter.shape[0]
    pair_count = chan_count // 2
    tails = jnp.stack([query_proj[:, -2:], key_proj[:, -2:], value_proj[:, -2:]])
    before = shifted(tails, "ctx", 1)
    q_conv = causal_three(query_proj, before[0], short_taps[0])
    k_conv = causal_three(key_proj, before[1], short_taps[1])
    v_conv = causal_three(value_proj, before[2], short_taps[2])
    product = k_conv * v_conv
    halves = product.reshape(filter_count, 2, -1, tok_count)
    both_in = jnp.concatenate(
        [
            halves[:, 0].reshape(pair_count, tok_count),
            long_filter,
            halves[:, 1].reshape(pair_count, tok_count),
            jnp.zeros_like(long_filter),
        ],
        axis=0,
    )
    row_total = pair_count + filter_count
    moved = lax.all_to_all(
        both_in.reshape(2 * row_total, row_count, ctx_count), "ctx", split_axis=2, concat_axis=1,
        tiled=True,
    )
    moved = moved.reshape(2 * row_total, row_count, ctx_count)
    spec_real, spec_imag = forward_local(
        moved[:row_total], moved[row_total:], first_len, ctx_count, ctx_index
    )
    spec = lax.all_to_all(
        jnp.concatenate([spec_real, spec_imag], axis=0), "ctx", split_axis=2, concat_axis=2,
        tiled=True,
    )
    square_tables = grid_product(ctx_count, ctx_count, ctx_count)
    spec_real, spec_imag = dft_section(
        apply_cols, spec[:row_total], spec[row_total:], square_tables, -1.0
    )
    data_real = spec_real[:pair_count]
    data_imag = spec_imag[:pair_count]
    filt_real = spec_real[pair_count:]
    filt_imag = spec_imag[pair_count:]
    grouped_shape = (filter_count, pair_count // filter_count, first_len, ctx_count)
    group_real = data_real.reshape(grouped_shape)
    group_imag = data_imag.reshape(grouped_shape)
    prod_real = (group_real * filt_real[:, None] - group_imag * filt_imag[:, None]).reshape(
        data_real.shape
    )
    prod_imag = (group_real * filt_imag[:, None] + group_imag * filt_real[:, None]).reshape(
        data_real.shape
    )
    back_real, back_imag = dft_section(apply_cols, prod_real, prod_imag, square_tables, 1.0)
    freq_first = lax.broadcasted_iota(jnp.int32, (first_len, ctx_count), 0)
    time_third = lax.broadcasted_iota(jnp.int32, (first_len, ctx_count), 1)
    twist = trig_pair((freq_first + first_len * ctx_index) * time_third, padded_len)
    back_real, back_imag = rotate(back_real, back_imag, twist, 1.0)
    back = lax.all_to_all(
        jnp.concatenate([back_real, back_imag], axis=0), "ctx", split_axis=2, concat_axis=2,
        tiled=True,
    )
    back_real, back_imag = dft_section(
        apply_cols, back[:pair_count], back[pair_count:], square_tables, 1.0
    )
    back_real, back_imag = rotate(
        back_real, back_imag, grid_product(first_len, ctx_count, first_len * ctx_count), 1.0
    )
    last_tables = grid_product(row_count, first_len, first_len)
    time_real, time_imag = dft_section(apply_rows, back_real, back_imag, last_tables, 1.0)
    time_vals = jnp.concatenate([time_real, time_imag], axis=0)
    time_vals = time_vals.reshape(chan_count, row_count * ctx_count, 1) * (1.0 / padded_len)
    convolved = lax.all_to_all(time_vals, "ctx", split_axis=1, concat_axis=2, tiled=True)
    convolved = convolved.reshape(2, filter_count, -1, tok_count).transpose(1, 0, 2, 3)
    convolved = convolved.reshape(chan_count, tok_count)
    mixed = q_conv * (convolved + skip_scale[:, None] * product)
    power = lax.psum(jnp.sum(mixed * mixed, axis=0), "tp")
    total_channels = chan_count * lax.axis_size("tp")
    return (norm_gain[:, None] * mixed * lax.rsqrt(power / total_channels + 1e-05)).astype(
        jnp.bfloat16
    )


def solution(mesh):
    return jax.shard_map(
        shards,
        mesh=mesh,
        in_specs=(
            P("tp", "ctx"),
            P("tp", "ctx"),
            P("tp", "ctx"),
            P(None, "tp", None),
            P("tp", "ctx"),
            P("tp"),
            P("tp"),
        ),
        out_specs=P("tp", "ctx"),
        check_vma=False,
    )
```

```python
import math

import jax
import jax.numpy as jnp
from jax import lax
from jax.sharding import PartitionSpec as P

HIGHEST = lax.Precision.HIGHEST


def shifted(x, axis, by):
    length = lax.axis_size(axis)
    pairs = [(i, i + by) for i in range(length) if 0 <= i + by < length]
    return lax.ppermute(x, axis, pairs)


def trig_pair(steps_int, modulus):
    angle = (steps_int % modulus).astype(jnp.float32) * (2.0 * math.pi / modulus)
    return (jnp.cos(angle), jnp.sin(angle))


def grid_product(first_len, second_len, modulus):
    left = lax.broadcasted_iota(jnp.int32, (first_len, second_len), 0)
    right = lax.broadcasted_iota(jnp.int32, (first_len, second_len), 1)
    return trig_pair(left * right, modulus)


def apply_rows(table, values):
    return jnp.einsum("kt,ctn->ckn", table, values, precision=HIGHEST)


def apply_cols(table, values):
    return jnp.einsum("ckn,nm->ckm", values, table, precision=HIGHEST)


def dft_section(apply_fn, real_part, imag_part, tables, direction):
    cos_table, sin_table = tables
    if imag_part is None:
        return (apply_fn(cos_table, real_part), direction * apply_fn(sin_table, real_part))
    if apply_fn is apply_cols:
        block = jnp.concatenate(
            [
                jnp.concatenate([cos_table, direction * sin_table], axis=1),
                jnp.concatenate([-direction * sin_table, cos_table], axis=1),
            ],
            axis=0,
        )
        both = apply_cols(block, jnp.concatenate([real_part, imag_part], axis=2))
        out_len = cos_table.shape[1]
        return (both[:, :, :out_len], both[:, :, out_len:])
    block = jnp.concatenate(
        [
            jnp.concatenate([cos_table, -direction * sin_table], axis=1),
            jnp.concatenate([direction * sin_table, cos_table], axis=1),
        ],
        axis=0,
    )
    both = apply_rows(block, jnp.concatenate([real_part, imag_part], axis=1))
    out_len = cos_table.shape[0]
    return (both[:, :out_len], both[:, out_len:])


def rotate(real_part, imag_part, tables, direction):
    cos_table, sin_table = tables
    new_real = real_part * cos_table - direction * imag_part * sin_table
    new_imag = direction * real_part * sin_table + imag_part * cos_table
    return (new_real, new_imag)


def forward_local(real_part, imag_part, first_len, ctx_count, ctx_index):
    rows_real = real_part.shape[1]
    padded_len = first_len * ctx_count * ctx_count
    first_tables = grid_product(first_len, rows_real, first_len)
    real_part, imag_part = dft_section(apply_rows, real_part, imag_part, first_tables, -1.0)
    real_part, imag_part = rotate(
        real_part, imag_part, grid_product(first_len, ctx_count, first_len * ctx_count), -1.0
    )
    real_part, imag_part = dft_section(
        apply_cols, real_part, imag_part, grid_product(ctx_count, ctx_count, ctx_count), -1.0
    )
    freq_first = lax.broadcasted_iota(jnp.int32, (first_len, ctx_count), 0)
    freq_second = lax.broadcasted_iota(jnp.int32, (first_len, ctx_count), 1)
    twist = trig_pair((freq_first + first_len * freq_second) * ctx_index, padded_len)
    return rotate(real_part, imag_part, twist, -1.0)


def causal_three(values, before, taps):
    extended = jnp.concatenate([before.astype(jnp.float32), values.astype(jnp.float32)], axis=1)
    return (
        taps[:, 0:1] * extended[:, 2:]
        + taps[:, 1:2] * extended[:, 1:-1]
        + taps[:, 2:3] * extended[:, :-2]
    )


def shards(query_proj, key_proj, value_proj, short_taps, long_filter, skip_scale, norm_gain):
    chan_count = query_proj.shape[0]
    tok_count = query_proj.shape[1]
    ctx_count = lax.axis_size("ctx")
    ctx_index = lax.axis_index("ctx")
    row_count = tok_count // ctx_count
    first_len = 2 * row_count
    padded_len = first_len * ctx_count * ctx_count
    filter_count = long_filter.shape[0]
    pair_count = chan_count // 2
    tails = jnp.stack([query_proj[:, -2:], key_proj[:, -2:], value_proj[:, -2:]])
    before = shifted(tails, "ctx", 1)
    q_conv = causal_three(query_proj, before[0], short_taps[0])
    k_conv = causal_three(key_proj, before[1], short_taps[1])
    v_conv = causal_three(value_proj, before[2], short_taps[2])
    product = k_conv * v_conv
    halves = product.reshape(filter_count, 2, -1, tok_count)
    both_in = jnp.concatenate(
        [
            halves[:, 0].reshape(pair_count, tok_count),
            long_filter,
            halves[:, 1].reshape(pair_count, tok_count),
            jnp.zeros_like(long_filter),
        ],
        axis=0,
    )
    row_total = pair_count + filter_count
    skip_part = skip_scale[:, None] * product
    gated_q = norm_gain[:, None] * q_conv
    both_in, skip_part, gated_q, q_conv = lax.optimization_barrier(
        (both_in, skip_part, gated_q, q_conv)
    )
    moved = lax.all_to_all(
        both_in.reshape(2 * row_total, row_count, ctx_count), "ctx", split_axis=2, concat_axis=1,
        tiled=True,
    )
    moved = moved.reshape(2 * row_total, row_count, ctx_count)
    spec_real, spec_imag = forward_local(
        moved[:row_total], moved[row_total:], first_len, ctx_count, ctx_index
    )
    spec = lax.all_to_all(
        jnp.concatenate([spec_real, spec_imag], axis=0), "ctx", split_axis=2, concat_axis=2,
        tiled=True,
    )
    square_tables = grid_product(ctx_count, ctx_count, ctx_count)
    spec_real, spec_imag = dft_section(
        apply_cols, spec[:row_total], spec[row_total:], square_tables, -1.0
    )
    data_real = spec_real[:pair_count]
    data_imag = spec_imag[:pair_count]
    filt_real = spec_real[pair_count:]
    filt_imag = spec_imag[pair_count:]
    grouped_shape = (filter_count, pair_count // filter_count, first_len, ctx_count)
    group_real = data_real.reshape(grouped_shape)
    group_imag = data_imag.reshape(grouped_shape)
    prod_real = (group_real * filt_real[:, None] - group_imag * filt_imag[:, None]).reshape(
        data_real.shape
    )
    prod_imag = (group_real * filt_imag[:, None] + group_imag * filt_real[:, None]).reshape(
        data_real.shape
    )
    back_real, back_imag = dft_section(apply_cols, prod_real, prod_imag, square_tables, 1.0)
    freq_first = lax.broadcasted_iota(jnp.int32, (first_len, ctx_count), 0)
    time_third = lax.broadcasted_iota(jnp.int32, (first_len, ctx_count), 1)
    twist = trig_pair((freq_first + first_len * ctx_index) * time_third, padded_len)
    back_real, back_imag = rotate(back_real, back_imag, twist, 1.0)
    back = lax.all_to_all(
        jnp.concatenate([back_real, back_imag], axis=0), "ctx", split_axis=2, concat_axis=2,
        tiled=True,
    )
    back_real, back_imag = dft_section(
        apply_cols, back[:pair_count], back[pair_count:], square_tables, 1.0
    )
    back_real, back_imag = rotate(
        back_real, back_imag, grid_product(first_len, ctx_count, first_len * ctx_count), 1.0
    )
    last_tables = grid_product(row_count, first_len, first_len)
    time_real, time_imag = dft_section(apply_rows, back_real, back_imag, last_tables, 1.0)
    time_vals = jnp.concatenate([time_real, time_imag], axis=0)
    time_vals = time_vals.reshape(chan_count, row_count * ctx_count, 1) * (1.0 / padded_len)
    convolved = lax.all_to_all(time_vals, "ctx", split_axis=1, concat_axis=2, tiled=True)
    convolved = convolved.reshape(2, filter_count, -1, tok_count).transpose(1, 0, 2, 3)
    convolved = convolved.reshape(chan_count, tok_count)
    gate = convolved + skip_part
    mixed = q_conv * gate
    power = lax.psum(jnp.sum(mixed * mixed, axis=0), "tp")
    total_channels = chan_count * lax.axis_size("tp")
    return (gated_q * gate * lax.rsqrt(power / total_channels + 1e-05)).astype(jnp.bfloat16)


def solution(mesh):
    return jax.shard_map(
        shards,
        mesh=mesh,
        in_specs=(
            P("tp", "ctx"),
            P("tp", "ctx"),
            P("tp", "ctx"),
            P(None, "tp", None),
            P("tp", "ctx"),
            P("tp"),
            P("tp"),
        ),
        out_specs=P("tp", "ctx"),
        check_vma=False,
    )
```

```python
import math

import jax
import jax.numpy as jnp
from jax import lax
from jax.sharding import PartitionSpec as P

HIGHEST = lax.Precision.HIGHEST


def shifted(x, axis, by):
    length = lax.axis_size(axis)
    pairs = [(i, i + by) for i in range(length) if 0 <= i + by < length]
    return lax.ppermute(x, axis, pairs)


def trig_pair(steps_int, modulus):
    angle = (steps_int % modulus).astype(jnp.float32) * (2.0 * math.pi / modulus)
    return (jnp.cos(angle), jnp.sin(angle))


def grid_product(first_len, second_len, modulus):
    left = lax.broadcasted_iota(jnp.int32, (first_len, second_len), 0)
    right = lax.broadcasted_iota(jnp.int32, (first_len, second_len), 1)
    return trig_pair(left * right, modulus)


def apply_rows(table, values):
    return jnp.einsum("kt,ctn->ckn", table, values, precision=HIGHEST)


def apply_cols(table, values):
    return jnp.einsum("ckn,nm->ckm", values, table, precision=HIGHEST)


def dft_section(apply_fn, real_part, imag_part, tables, direction):
    cos_table, sin_table = tables
    if imag_part is None:
        return (apply_fn(cos_table, real_part), direction * apply_fn(sin_table, real_part))
    if apply_fn is apply_cols:
        block = jnp.concatenate(
            [
                jnp.concatenate([cos_table, direction * sin_table], axis=1),
                jnp.concatenate([-direction * sin_table, cos_table], axis=1),
            ],
            axis=0,
        )
        both = apply_cols(block, jnp.concatenate([real_part, imag_part], axis=2))
        out_len = cos_table.shape[1]
        return (both[:, :, :out_len], both[:, :, out_len:])
    block = jnp.concatenate(
        [
            jnp.concatenate([cos_table, -direction * sin_table], axis=1),
            jnp.concatenate([direction * sin_table, cos_table], axis=1),
        ],
        axis=0,
    )
    both = apply_rows(block, jnp.concatenate([real_part, imag_part], axis=1))
    out_len = cos_table.shape[0]
    return (both[:, :out_len], both[:, out_len:])


def rotate(real_part, imag_part, tables, direction):
    cos_table, sin_table = tables
    new_real = real_part * cos_table - direction * imag_part * sin_table
    new_imag = direction * real_part * sin_table + imag_part * cos_table
    return (new_real, new_imag)


def forward_local(real_part, imag_part, first_len, ctx_count, ctx_index):
    rows_real = real_part.shape[1]
    padded_len = first_len * ctx_count * ctx_count
    first_tables = grid_product(first_len, rows_real, first_len)
    real_part, imag_part = dft_section(apply_rows, real_part, imag_part, first_tables, -1.0)
    real_part, imag_part = rotate(
        real_part, imag_part, grid_product(first_len, ctx_count, first_len * ctx_count), -1.0
    )
    real_part, imag_part = dft_section(
        apply_cols, real_part, imag_part, grid_product(ctx_count, ctx_count, ctx_count), -1.0
    )
    freq_first = lax.broadcasted_iota(jnp.int32, (first_len, ctx_count), 0)
    freq_second = lax.broadcasted_iota(jnp.int32, (first_len, ctx_count), 1)
    twist = trig_pair((freq_first + first_len * freq_second) * ctx_index, padded_len)
    return rotate(real_part, imag_part, twist, -1.0)


def causal_three(values, before, taps):
    extended = jnp.concatenate([before.astype(jnp.float32), values.astype(jnp.float32)], axis=1)
    return (
        taps[:, 0:1] * extended[:, 2:]
        + taps[:, 1:2] * extended[:, 1:-1]
        + taps[:, 2:3] * extended[:, :-2]
    )


def shards(query_proj, key_proj, value_proj, short_taps, long_filter, skip_scale, norm_gain):
    chan_count = query_proj.shape[0]
    tok_count = query_proj.shape[1]
    ctx_count = lax.axis_size("ctx")
    ctx_index = lax.axis_index("ctx")
    row_count = tok_count // ctx_count
    first_len = 2 * row_count
    padded_len = first_len * ctx_count * ctx_count
    filter_count = long_filter.shape[0]
    pair_count = chan_count // 2
    tails = jnp.stack([query_proj[:, -2:], key_proj[:, -2:], value_proj[:, -2:]])
    before = shifted(tails, "ctx", 1)
    q_conv = causal_three(query_proj, before[0], short_taps[0])
    k_conv = causal_three(key_proj, before[1], short_taps[1])
    v_conv = causal_three(value_proj, before[2], short_taps[2])
    product = k_conv * v_conv
    halves = product.reshape(filter_count, 2, -1, tok_count)
    both_in = jnp.concatenate(
        [
            halves[:, 0].reshape(pair_count, tok_count),
            long_filter,
            halves[:, 1].reshape(pair_count, tok_count),
            jnp.zeros_like(long_filter),
        ],
        axis=0,
    )
    row_total = pair_count + filter_count
    moved = lax.all_to_all(
        both_in.reshape(2 * row_total, row_count, ctx_count), "ctx", split_axis=2, concat_axis=1,
        tiled=True,
    )
    moved = moved.reshape(2 * row_total, row_count, ctx_count)
    spec_real, spec_imag = forward_local(
        moved[:row_total], moved[row_total:], first_len, ctx_count, ctx_index
    )
    spec = lax.all_to_all(
        jnp.concatenate([spec_real, spec_imag], axis=0), "ctx", split_axis=2, concat_axis=2,
        tiled=True,
    )
    square_tables = grid_product(ctx_count, ctx_count, ctx_count)
    spec_real, spec_imag = dft_section(
        apply_cols, spec[:row_total], spec[row_total:], square_tables, -1.0
    )
    data_real = spec_real[:pair_count]
    data_imag = spec_imag[:pair_count]
    filt_real = spec_real[pair_count:]
    filt_imag = spec_imag[pair_count:]
    grouped_shape = (filter_count, pair_count // filter_count, first_len, ctx_count)
    group_real = data_real.reshape(grouped_shape)
    group_imag = data_imag.reshape(grouped_shape)
    prod_real = (group_real * filt_real[:, None] - group_imag * filt_imag[:, None]).reshape(
        data_real.shape
    )
    prod_imag = (group_real * filt_imag[:, None] + group_imag * filt_real[:, None]).reshape(
        data_real.shape
    )
    back_real, back_imag = dft_section(apply_cols, prod_real, prod_imag, square_tables, 1.0)
    freq_first = lax.broadcasted_iota(jnp.int32, (first_len, ctx_count), 0)
    time_third = lax.broadcasted_iota(jnp.int32, (first_len, ctx_count), 1)
    twist = trig_pair((freq_first + first_len * ctx_index) * time_third, padded_len)
    back_real, back_imag = rotate(back_real, back_imag, twist, 1.0)
    back = lax.all_to_all(
        jnp.concatenate([back_real, back_imag], axis=0), "ctx", split_axis=2, concat_axis=2,
        tiled=True,
    )
    back_real, back_imag = dft_section(
        apply_cols, back[:pair_count], back[pair_count:], square_tables, 1.0
    )
    back_real, back_imag = rotate(
        back_real, back_imag, grid_product(first_len, ctx_count, first_len * ctx_count), 1.0
    )
    last_cos, last_sin = grid_product(row_count, first_len, first_len)
    last_block = jnp.concatenate(
        [
            jnp.concatenate([last_cos, -last_sin], axis=1),
            jnp.concatenate([last_sin, last_cos], axis=1),
        ],
        axis=0,
    )
    time_vals = jnp.einsum(
        "ut,ctq->uqc", last_block, jnp.concatenate([back_real, back_imag], axis=1),
        precision=HIGHEST,
    )
    time_vals = time_vals.reshape(2, row_count, ctx_count, pair_count).transpose(1, 2, 0, 3)
    time_vals = time_vals.reshape(ctx_count, tok_count // ctx_count, chan_count)
    time_vals = time_vals * (1.0 / padded_len)
    convolved = lax.all_to_all(time_vals, "ctx", split_axis=0, concat_axis=0, tiled=True)
    convolved = convolved.transpose(2, 1, 0).reshape(2, filter_count, -1, tok_count)
    convolved = convolved.transpose(1, 0, 2, 3).reshape(chan_count, tok_count)
    mixed = q_conv * (convolved + skip_scale[:, None] * product)
    power = lax.psum(jnp.sum(mixed * mixed, axis=0), "tp")
    total_channels = chan_count * lax.axis_size("tp")
    return (norm_gain[:, None] * mixed * lax.rsqrt(power / total_channels + 1e-05)).astype(
        jnp.bfloat16
    )


def solution(mesh):
    return jax.shard_map(
        shards,
        mesh=mesh,
        in_specs=(
            P("tp", "ctx"),
            P("tp", "ctx"),
            P("tp", "ctx"),
            P(None, "tp", None),
            P("tp", "ctx"),
            P("tp"),
            P("tp"),
        ),
        out_specs=P("tp", "ctx"),
        check_vma=False,
    )
```

```python
import math

import jax
import jax.numpy as jnp
from jax import lax
from jax.sharding import PartitionSpec as P

HIGHEST = lax.Precision.HIGHEST


def shifted(x, axis, by):
    length = lax.axis_size(axis)
    pairs = [(i, i + by) for i in range(length) if 0 <= i + by < length]
    return lax.ppermute(x, axis, pairs)


def trig_pair(steps_int, modulus):
    angle = (steps_int % modulus).astype(jnp.float32) * (2.0 * math.pi / modulus)
    return (jnp.cos(angle), jnp.sin(angle))


def grid_product(first_len, second_len, modulus):
    left = lax.broadcasted_iota(jnp.int32, (first_len, second_len), 0)
    right = lax.broadcasted_iota(jnp.int32, (first_len, second_len), 1)
    return trig_pair(left * right, modulus)


def apply_rows(table, values):
    return jnp.einsum("kt,ctn->ckn", table, values, precision=HIGHEST)


def apply_cols(table, values):
    return jnp.einsum("ckn,nm->ckm", values, table, precision=HIGHEST)


def dft_section(apply_fn, real_part, imag_part, tables, direction):
    cos_table, sin_table = tables
    if imag_part is None:
        return (apply_fn(cos_table, real_part), direction * apply_fn(sin_table, real_part))
    if apply_fn is apply_cols:
        block = jnp.concatenate(
            [
                jnp.concatenate([cos_table, direction * sin_table], axis=1),
                jnp.concatenate([-direction * sin_table, cos_table], axis=1),
            ],
            axis=0,
        )
        both = apply_cols(block, jnp.concatenate([real_part, imag_part], axis=2))
        out_len = cos_table.shape[1]
        return (both[:, :, :out_len], both[:, :, out_len:])
    block = jnp.concatenate(
        [
            jnp.concatenate([cos_table, -direction * sin_table], axis=1),
            jnp.concatenate([direction * sin_table, cos_table], axis=1),
        ],
        axis=0,
    )
    both = apply_rows(block, jnp.concatenate([real_part, imag_part], axis=1))
    out_len = cos_table.shape[0]
    return (both[:, :out_len], both[:, out_len:])


def rotate(real_part, imag_part, tables, direction):
    cos_table, sin_table = tables
    new_real = real_part * cos_table - direction * imag_part * sin_table
    new_imag = direction * real_part * sin_table + imag_part * cos_table
    return (new_real, new_imag)


def forward_local(real_part, imag_part, first_len, ctx_count, ctx_index):
    rows_real = real_part.shape[1]
    padded_len = first_len * ctx_count * ctx_count
    first_tables = grid_product(first_len, rows_real, first_len)
    real_part, imag_part = dft_section(apply_rows, real_part, imag_part, first_tables, -1.0)
    real_part, imag_part = rotate(
        real_part, imag_part, grid_product(first_len, ctx_count, first_len * ctx_count), -1.0
    )
    real_part, imag_part = dft_section(
        apply_cols, real_part, imag_part, grid_product(ctx_count, ctx_count, ctx_count), -1.0
    )
    freq_first = lax.broadcasted_iota(jnp.int32, (first_len, ctx_count), 0)
    freq_second = lax.broadcasted_iota(jnp.int32, (first_len, ctx_count), 1)
    twist = trig_pair((freq_first + first_len * freq_second) * ctx_index, padded_len)
    return rotate(real_part, imag_part, twist, -1.0)


def causal_three(values, before, taps):
    extended = jnp.concatenate([before.astype(jnp.float32), values.astype(jnp.float32)], axis=1)
    return (
        taps[:, 0:1] * extended[:, 2:]
        + taps[:, 1:2] * extended[:, 1:-1]
        + taps[:, 2:3] * extended[:, :-2]
    )


def shards(query_proj, key_proj, value_proj, short_taps, long_filter, skip_scale, norm_gain):
    chan_count = query_proj.shape[0]
    tok_count = query_proj.shape[1]
    ctx_count = lax.axis_size("ctx")
    ctx_index = lax.axis_index("ctx")
    row_count = tok_count // ctx_count
    first_len = 2 * row_count
    padded_len = first_len * ctx_count * ctx_count
    filter_count = long_filter.shape[0]
    pair_count = chan_count // 2
    tails = jnp.stack([query_proj[:, -2:], key_proj[:, -2:], value_proj[:, -2:]])
    before = shifted(tails, "ctx", 1)
    q_conv = causal_three(query_proj, before[0], short_taps[0])
    k_conv = causal_three(key_proj, before[1], short_taps[1])
    v_conv = causal_three(value_proj, before[2], short_taps[2])
    product = k_conv * v_conv
    halves = product.reshape(filter_count, 2, -1, tok_count)
    both_in = jnp.concatenate(
        [
            halves[:, 0].reshape(pair_count, tok_count),
            long_filter,
            halves[:, 1].reshape(pair_count, tok_count),
            jnp.zeros_like(long_filter),
        ],
        axis=0,
    )
    row_total = pair_count + filter_count
    moved = lax.all_to_all(
        both_in.reshape(2 * row_total, row_count, ctx_count), "ctx", split_axis=2, concat_axis=1,
        tiled=True,
    )
    moved = moved.reshape(2 * row_total, row_count, ctx_count)
    spec_real, spec_imag = forward_local(
        moved[:row_total], moved[row_total:], first_len, ctx_count, ctx_index
    )
    spec = lax.all_to_all(
        jnp.concatenate([spec_real, spec_imag], axis=0), "ctx", split_axis=2, concat_axis=2,
        tiled=True,
    )
    square_tables = grid_product(ctx_count, ctx_count, ctx_count)
    spec_real, spec_imag = dft_section(
        apply_cols, spec[:row_total], spec[row_total:], square_tables, -1.0
    )
    data_real = spec_real[:pair_count]
    data_imag = spec_imag[:pair_count]
    filt_real = spec_real[pair_count:]
    filt_imag = spec_imag[pair_count:]
    grouped_shape = (filter_count, pair_count // filter_count, first_len, ctx_count)
    group_real = data_real.reshape(grouped_shape)
    group_imag = data_imag.reshape(grouped_shape)
    prod_real = (group_real * filt_real[:, None] - group_imag * filt_imag[:, None]).reshape(
        data_real.shape
    )
    prod_imag = (group_real * filt_imag[:, None] + group_imag * filt_real[:, None]).reshape(
        data_real.shape
    )
    back_real, back_imag = dft_section(apply_cols, prod_real, prod_imag, square_tables, 1.0)
    freq_first = lax.broadcasted_iota(jnp.int32, (first_len, ctx_count), 0)
    time_third = lax.broadcasted_iota(jnp.int32, (first_len, ctx_count), 1)
    twist = trig_pair((freq_first + first_len * ctx_index) * time_third, padded_len)
    back_real, back_imag = rotate(back_real, back_imag, twist, 1.0)
    back = lax.all_to_all(
        jnp.concatenate([back_real, back_imag], axis=0), "ctx", split_axis=2, concat_axis=2,
        tiled=True,
    )
    back_real, back_imag = dft_section(
        apply_cols, back[:pair_count], back[pair_count:], square_tables, 1.0
    )
    back_real, back_imag = rotate(
        back_real, back_imag, grid_product(first_len, ctx_count, first_len * ctx_count), 1.0
    )
    last_cos, last_sin = grid_product(row_count, first_len, first_len)
    last_block = jnp.concatenate(
        [
            jnp.concatenate([last_cos, -last_sin], axis=1),
            jnp.concatenate([last_sin, last_cos], axis=1),
        ],
        axis=0,
    ) * (1.0 / padded_len)
    time_vals = jnp.einsum(
        "ut,ctq->uqc", last_block, jnp.concatenate([back_real, back_imag], axis=1),
        precision=HIGHEST,
    )
    time_vals = time_vals.reshape(2, row_count, ctx_count, pair_count).transpose(1, 2, 0, 3)
    time_vals = time_vals.reshape(ctx_count, tok_count // ctx_count, chan_count)
    convolved = lax.all_to_all(time_vals, "ctx", split_axis=0, concat_axis=0, tiled=True)
    convolved = convolved.transpose(2, 1, 0).reshape(2, filter_count, -1, tok_count)
    convolved = convolved.transpose(1, 0, 2, 3).reshape(chan_count, tok_count)
    mixed = q_conv * (convolved + skip_scale[:, None] * product)
    power = lax.psum(jnp.sum(mixed * mixed, axis=0), "tp")
    total_channels = chan_count * lax.axis_size("tp")
    return (norm_gain[:, None] * mixed * lax.rsqrt(power / total_channels + 1e-05)).astype(
        jnp.bfloat16
    )


def solution(mesh):
    return jax.shard_map(
        shards,
        mesh=mesh,
        in_specs=(
            P("tp", "ctx"),
            P("tp", "ctx"),
            P("tp", "ctx"),
            P(None, "tp", None),
            P("tp", "ctx"),
            P("tp"),
            P("tp"),
        ),
        out_specs=P("tp", "ctx"),
        check_vma=False,
    )
```

```python
import math

import jax
import jax.numpy as jnp
from jax import lax
from jax.sharding import PartitionSpec as P

HIGHEST = lax.Precision.HIGHEST


def shifted(x, axis, by):
    length = lax.axis_size(axis)
    pairs = [(i, i + by) for i in range(length) if 0 <= i + by < length]
    return lax.ppermute(x, axis, pairs)


def trig_pair(steps_int, modulus):
    angle = (steps_int % modulus).astype(jnp.float32) * (2.0 * math.pi / modulus)
    return (jnp.cos(angle), jnp.sin(angle))


def grid_product(first_len, second_len, modulus):
    left = lax.broadcasted_iota(jnp.int32, (first_len, second_len), 0)
    right = lax.broadcasted_iota(jnp.int32, (first_len, second_len), 1)
    return trig_pair(left * right, modulus)


def apply_rows(table, values):
    return jnp.einsum("kt,ctn->ckn", table, values, precision=HIGHEST)


def apply_cols(table, values):
    return jnp.einsum("ckn,nm->ckm", values, table, precision=HIGHEST)


def dft_section(apply_fn, real_part, imag_part, tables, direction):
    cos_table, sin_table = tables
    if imag_part is None:
        return (apply_fn(cos_table, real_part), direction * apply_fn(sin_table, real_part))
    if apply_fn is apply_cols:
        block = jnp.concatenate(
            [
                jnp.concatenate([cos_table, direction * sin_table], axis=1),
                jnp.concatenate([-direction * sin_table, cos_table], axis=1),
            ],
            axis=0,
        )
        both = apply_cols(block, jnp.concatenate([real_part, imag_part], axis=2))
        out_len = cos_table.shape[1]
        return (both[:, :, :out_len], both[:, :, out_len:])
    block = jnp.concatenate(
        [
            jnp.concatenate([cos_table, -direction * sin_table], axis=1),
            jnp.concatenate([direction * sin_table, cos_table], axis=1),
        ],
        axis=0,
    )
    both = apply_rows(block, jnp.concatenate([real_part, imag_part], axis=1))
    out_len = cos_table.shape[0]
    return (both[:, :out_len], both[:, out_len:])


def rotate(real_part, imag_part, tables, direction):
    cos_table, sin_table = tables
    new_real = real_part * cos_table - direction * imag_part * sin_table
    new_imag = direction * real_part * sin_table + imag_part * cos_table
    return (new_real, new_imag)


def forward_local(real_part, imag_part, first_len, ctx_count, ctx_index):
    rows_real = real_part.shape[1]
    padded_len = first_len * ctx_count * ctx_count
    first_tables = grid_product(first_len, rows_real, first_len)
    real_part, imag_part = dft_section(apply_rows, real_part, imag_part, first_tables, -1.0)
    real_part, imag_part = rotate(
        real_part, imag_part, grid_product(first_len, ctx_count, first_len * ctx_count), -1.0
    )
    real_part, imag_part = dft_section(
        apply_cols, real_part, imag_part, grid_product(ctx_count, ctx_count, ctx_count), -1.0
    )
    freq_first = lax.broadcasted_iota(jnp.int32, (first_len, ctx_count), 0)
    freq_second = lax.broadcasted_iota(jnp.int32, (first_len, ctx_count), 1)
    twist = trig_pair((freq_first + first_len * freq_second) * ctx_index, padded_len)
    return rotate(real_part, imag_part, twist, -1.0)


def causal_three(values, before, taps):
    extended = jnp.concatenate([before.astype(jnp.float32), values.astype(jnp.float32)], axis=1)
    return (
        taps[:, 0:1] * extended[:, 2:]
        + taps[:, 1:2] * extended[:, 1:-1]
        + taps[:, 2:3] * extended[:, :-2]
    )


def shards(query_proj, key_proj, value_proj, short_taps, long_filter, skip_scale, norm_gain):
    chan_count = query_proj.shape[0]
    tok_count = query_proj.shape[1]
    ctx_count = lax.axis_size("ctx")
    ctx_index = lax.axis_index("ctx")
    row_count = tok_count // ctx_count
    first_len = 2 * row_count
    padded_len = first_len * ctx_count * ctx_count
    filter_count = long_filter.shape[0]
    pair_count = chan_count // 2
    tails = jnp.stack([query_proj[:, -2:], key_proj[:, -2:], value_proj[:, -2:]])
    before = shifted(tails, "ctx", 1)
    q_conv = causal_three(query_proj, before[0], short_taps[0])
    k_conv = causal_three(key_proj, before[1], short_taps[1])
    v_conv = causal_three(value_proj, before[2], short_taps[2])
    product = k_conv * v_conv
    halves = product.reshape(filter_count, 2, -1, tok_count)
    both_in = jnp.concatenate(
        [
            halves[:, 0].reshape(pair_count, tok_count),
            long_filter,
            halves[:, 1].reshape(pair_count, tok_count),
            jnp.zeros_like(long_filter),
        ],
        axis=0,
    )
    row_total = pair_count + filter_count
    both_in, scales = lax.optimization_barrier((both_in, jnp.stack([skip_scale, norm_gain])))
    moved = lax.all_to_all(
        both_in.reshape(2 * row_total, row_count, ctx_count), "ctx", split_axis=2, concat_axis=1,
        tiled=True,
    )
    moved = moved.reshape(2 * row_total, row_count, ctx_count)
    spec_real, spec_imag = forward_local(
        moved[:row_total], moved[row_total:], first_len, ctx_count, ctx_index
    )
    spec = lax.all_to_all(
        jnp.concatenate([spec_real, spec_imag], axis=0), "ctx", split_axis=2, concat_axis=2,
        tiled=True,
    )
    square_tables = grid_product(ctx_count, ctx_count, ctx_count)
    spec_real, spec_imag = dft_section(
        apply_cols, spec[:row_total], spec[row_total:], square_tables, -1.0
    )
    data_real = spec_real[:pair_count]
    data_imag = spec_imag[:pair_count]
    filt_real = spec_real[pair_count:]
    filt_imag = spec_imag[pair_count:]
    grouped_shape = (filter_count, pair_count // filter_count, first_len, ctx_count)
    group_real = data_real.reshape(grouped_shape)
    group_imag = data_imag.reshape(grouped_shape)
    prod_real = (group_real * filt_real[:, None] - group_imag * filt_imag[:, None]).reshape(
        data_real.shape
    )
    prod_imag = (group_real * filt_imag[:, None] + group_imag * filt_real[:, None]).reshape(
        data_real.shape
    )
    back_real, back_imag = dft_section(apply_cols, prod_real, prod_imag, square_tables, 1.0)
    freq_first = lax.broadcasted_iota(jnp.int32, (first_len, ctx_count), 0)
    time_third = lax.broadcasted_iota(jnp.int32, (first_len, ctx_count), 1)
    twist = trig_pair((freq_first + first_len * ctx_index) * time_third, padded_len)
    back_real, back_imag = rotate(back_real, back_imag, twist, 1.0)
    back = lax.all_to_all(
        jnp.concatenate([back_real, back_imag], axis=0), "ctx", split_axis=2, concat_axis=2,
        tiled=True,
    )
    back_real, back_imag = dft_section(
        apply_cols, back[:pair_count], back[pair_count:], square_tables, 1.0
    )
    back_real, back_imag = rotate(
        back_real, back_imag, grid_product(first_len, ctx_count, first_len * ctx_count), 1.0
    )
    last_cos, last_sin = grid_product(row_count, first_len, first_len)
    last_block = jnp.concatenate(
        [
            jnp.concatenate([last_cos, -last_sin], axis=1),
            jnp.concatenate([last_sin, last_cos], axis=1),
        ],
        axis=0,
    ) * (1.0 / padded_len)
    time_vals = jnp.einsum(
        "ut,ctq->uqc", last_block, jnp.concatenate([back_real, back_imag], axis=1),
        precision=HIGHEST,
    )
    time_vals = time_vals.reshape(2, row_count, ctx_count, pair_count).transpose(1, 2, 0, 3)
    time_vals = time_vals.reshape(ctx_count, tok_count // ctx_count, chan_count)
    convolved = lax.all_to_all(time_vals, "ctx", split_axis=0, concat_axis=0, tiled=True)
    convolved = convolved.transpose(2, 1, 0).reshape(2, filter_count, -1, tok_count)
    convolved = convolved.transpose(1, 0, 2, 3).reshape(chan_count, tok_count)
    mixed = q_conv * (convolved + scales[0][:, None] * product)
    power = lax.psum(jnp.sum(mixed * mixed, axis=0), "tp")
    total_channels = chan_count * lax.axis_size("tp")
    return (scales[1][:, None] * mixed * lax.rsqrt(power / total_channels + 1e-05)).astype(
        jnp.bfloat16
    )


def solution(mesh):
    return jax.shard_map(
        shards,
        mesh=mesh,
        in_specs=(
            P("tp", "ctx"),
            P("tp", "ctx"),
            P("tp", "ctx"),
            P(None, "tp", None),
            P("tp", "ctx"),
            P("tp"),
            P("tp"),
        ),
        out_specs=P("tp", "ctx"),
        check_vma=False,
    )
```

```python
import math

import jax
import jax.numpy as jnp
from jax import lax
from jax.sharding import PartitionSpec as P

HIGHEST = lax.Precision.HIGHEST


def shifted(x, axis, by):
    length = lax.axis_size(axis)
    pairs = [(i, i + by) for i in range(length) if 0 <= i + by < length]
    return lax.ppermute(x, axis, pairs)


def trig_pair(steps_int, modulus):
    angle = (steps_int % modulus).astype(jnp.float32) * (2.0 * math.pi / modulus)
    return (jnp.cos(angle), jnp.sin(angle))


def grid_product(first_len, second_len, modulus):
    left = lax.broadcasted_iota(jnp.int32, (first_len, second_len), 0)
    right = lax.broadcasted_iota(jnp.int32, (first_len, second_len), 1)
    return trig_pair(left * right, modulus)


def apply_rows(table, values):
    return jnp.einsum("kt,ctn->ckn", table, values, precision=HIGHEST)


def apply_cols(table, values):
    return jnp.einsum("ckn,nm->ckm", values, table, precision=HIGHEST)


def dft_section(apply_fn, real_part, imag_part, tables, direction):
    cos_table, sin_table = tables
    if imag_part is None:
        return (apply_fn(cos_table, real_part), direction * apply_fn(sin_table, real_part))
    if apply_fn is apply_cols:
        block = jnp.concatenate(
            [
                jnp.concatenate([cos_table, direction * sin_table], axis=1),
                jnp.concatenate([-direction * sin_table, cos_table], axis=1),
            ],
            axis=0,
        )
        both = apply_cols(block, jnp.concatenate([real_part, imag_part], axis=2))
        out_len = cos_table.shape[1]
        return (both[:, :, :out_len], both[:, :, out_len:])
    block = jnp.concatenate(
        [
            jnp.concatenate([cos_table, -direction * sin_table], axis=1),
            jnp.concatenate([direction * sin_table, cos_table], axis=1),
        ],
        axis=0,
    )
    both = apply_rows(block, jnp.concatenate([real_part, imag_part], axis=1))
    out_len = cos_table.shape[0]
    return (both[:, :out_len], both[:, out_len:])


def rotate(real_part, imag_part, tables, direction):
    cos_table, sin_table = tables
    new_real = real_part * cos_table - direction * imag_part * sin_table
    new_imag = direction * real_part * sin_table + imag_part * cos_table
    return (new_real, new_imag)


def forward_local(real_part, imag_part, first_len, ctx_count, ctx_index):
    rows_real = real_part.shape[1]
    padded_len = first_len * ctx_count * ctx_count
    first_tables = grid_product(first_len, rows_real, first_len)
    real_part, imag_part = dft_section(apply_rows, real_part, imag_part, first_tables, -1.0)
    real_part, imag_part = rotate(
        real_part, imag_part, grid_product(first_len, ctx_count, first_len * ctx_count), -1.0
    )
    cos_table, sin_table = grid_product(ctx_count, ctx_count, ctx_count)
    block = jnp.concatenate(
        [
            jnp.concatenate([cos_table, -sin_table], axis=1),
            jnp.concatenate([sin_table, cos_table], axis=1),
        ],
        axis=0,
    )
    both = jnp.einsum(
        "ckn,nm->mck", jnp.concatenate([real_part, imag_part], axis=2), block,
        precision=HIGHEST,
    )
    freq_second = lax.broadcasted_iota(jnp.int32, (ctx_count, 1, first_len), 0)
    freq_first = lax.broadcasted_iota(jnp.int32, (ctx_count, 1, first_len), 2)
    twist = trig_pair((freq_first + first_len * freq_second) * ctx_index, padded_len)
    real_part, imag_part = rotate(both[:ctx_count], both[ctx_count:], twist, -1.0)
    return jnp.stack([real_part, imag_part], axis=1).reshape(ctx_count, -1)


def causal_three(values, before, taps):
    extended = jnp.concatenate([before.astype(jnp.float32), values.astype(jnp.float32)], axis=1)
    return (
        taps[:, 0:1] * extended[:, 2:]
        + taps[:, 1:2] * extended[:, 1:-1]
        + taps[:, 2:3] * extended[:, :-2]
    )


def shards(query_proj, key_proj, value_proj, short_taps, long_filter, skip_scale, norm_gain):
    chan_count = query_proj.shape[0]
    tok_count = query_proj.shape[1]
    ctx_count = lax.axis_size("ctx")
    ctx_index = lax.axis_index("ctx")
    row_count = tok_count // ctx_count
    first_len = 2 * row_count
    padded_len = first_len * ctx_count * ctx_count
    filter_count = long_filter.shape[0]
    pair_count = chan_count // 2
    tails = jnp.stack([query_proj[:, -2:], key_proj[:, -2:], value_proj[:, -2:]])
    before = shifted(tails, "ctx", 1)
    q_conv = causal_three(query_proj, before[0], short_taps[0])
    k_conv = causal_three(key_proj, before[1], short_taps[1])
    v_conv = causal_three(value_proj, before[2], short_taps[2])
    product = k_conv * v_conv
    halves = product.reshape(filter_count, 2, -1, tok_count)
    both_in = jnp.concatenate(
        [
            halves[:, 0].reshape(pair_count, tok_count),
            long_filter,
            halves[:, 1].reshape(pair_count, tok_count),
            jnp.zeros_like(long_filter),
        ],
        axis=0,
    )
    row_total = pair_count + filter_count
    moved = lax.all_to_all(
        both_in.reshape(2 * row_total, row_count, ctx_count), "ctx", split_axis=2, concat_axis=1,
        tiled=True,
    )
    moved = moved.reshape(2 * row_total, row_count, ctx_count)
    spec = forward_local(moved[:row_total], moved[row_total:], first_len, ctx_count, ctx_index)
    spec = lax.all_to_all(spec, "ctx", split_axis=0, concat_axis=0, tiled=True)
    spec = spec.reshape(ctx_count, 2 * row_total, first_len).transpose(1, 2, 0)
    square_tables = grid_product(ctx_count, ctx_count, ctx_count)
    spec_real, spec_imag = dft_section(
        apply_cols, spec[:row_total], spec[row_total:], square_tables, -1.0
    )
    data_real = spec_real[:pair_count]
    data_imag = spec_imag[:pair_count]
    filt_real = spec_real[pair_count:]
    filt_imag = spec_imag[pair_count:]
    grouped_shape = (filter_count, pair_count // filter_count, first_len, ctx_count)
    group_real = data_real.reshape(grouped_shape)
    group_imag = data_imag.reshape(grouped_shape)
    prod_real = (group_real * filt_real[:, None] - group_imag * filt_imag[:, None]).reshape(
        data_real.shape
    )
    prod_imag = (group_real * filt_imag[:, None] + group_imag * filt_real[:, None]).reshape(
        data_real.shape
    )
    back_real, back_imag = dft_section(apply_cols, prod_real, prod_imag, square_tables, 1.0)
    freq_first = lax.broadcasted_iota(jnp.int32, (first_len, ctx_count), 0)
    time_third = lax.broadcasted_iota(jnp.int32, (first_len, ctx_count), 1)
    twist = trig_pair((freq_first + first_len * ctx_index) * time_third, padded_len)
    back_real, back_imag = rotate(back_real, back_imag, twist, 1.0)
    back = lax.all_to_all(
        jnp.concatenate([back_real, back_imag], axis=0), "ctx", split_axis=2, concat_axis=2,
        tiled=True,
    )
    back_real, back_imag = dft_section(
        apply_cols, back[:pair_count], back[pair_count:], square_tables, 1.0
    )
    back_real, back_imag = rotate(
        back_real, back_imag, grid_product(first_len, ctx_count, first_len * ctx_count), 1.0
    )
    last_cos, last_sin = grid_product(row_count, first_len, first_len)
    last_block = jnp.concatenate(
        [
            jnp.concatenate([last_cos, -last_sin], axis=1),
            jnp.concatenate([last_sin, last_cos], axis=1),
        ],
        axis=0,
    ) * (1.0 / padded_len)
    time_vals = jnp.einsum(
        "ut,ctq->uqc", last_block, jnp.concatenate([back_real, back_imag], axis=1),
        precision=HIGHEST,
    )
    time_vals = time_vals.reshape(2, row_count, ctx_count, pair_count).transpose(1, 2, 0, 3)
    time_vals = time_vals.reshape(ctx_count, tok_count // ctx_count, chan_count)
    convolved = lax.all_to_all(time_vals, "ctx", split_axis=0, concat_axis=0, tiled=True)
    convolved = convolved.transpose(2, 1, 0).reshape(2, filter_count, -1, tok_count)
    convolved = convolved.transpose(1, 0, 2, 3).reshape(chan_count, tok_count)
    mixed = q_conv * (convolved + skip_scale[:, None] * product)
    power = lax.psum(jnp.sum(mixed * mixed, axis=0), "tp")
    total_channels = chan_count * lax.axis_size("tp")
    return (norm_gain[:, None] * mixed * lax.rsqrt(power / total_channels + 1e-05)).astype(
        jnp.bfloat16
    )


def solution(mesh):
    return jax.shard_map(
        shards,
        mesh=mesh,
        in_specs=(
            P("tp", "ctx"),
            P("tp", "ctx"),
            P("tp", "ctx"),
            P(None, "tp", None),
            P("tp", "ctx"),
            P("tp"),
            P("tp"),
        ),
        out_specs=P("tp", "ctx"),
        check_vma=False,
    )
```

```python
import math

import jax
import jax.numpy as jnp
from jax import lax
from jax.sharding import PartitionSpec as P

HIGHEST = lax.Precision.HIGHEST


def shifted(x, axis, by):
    length = lax.axis_size(axis)
    pairs = [(i, i + by) for i in range(length) if 0 <= i + by < length]
    return lax.ppermute(x, axis, pairs)


def trig_pair(steps_int, modulus):
    angle = (steps_int % modulus).astype(jnp.float32) * (2.0 * math.pi / modulus)
    return (jnp.cos(angle), jnp.sin(angle))


def grid_product(first_len, second_len, modulus):
    left = lax.broadcasted_iota(jnp.int32, (first_len, second_len), 0)
    right = lax.broadcasted_iota(jnp.int32, (first_len, second_len), 1)
    return trig_pair(left * right, modulus)


def apply_rows(table, values):
    return jnp.einsum("kt,ctn->ckn", table, values, precision=HIGHEST)


def apply_cols(table, values):
    return jnp.einsum("ckn,nm->ckm", values, table, precision=HIGHEST)


def dft_section(apply_fn, real_part, imag_part, tables, direction):
    cos_table, sin_table = tables
    if imag_part is None:
        return (apply_fn(cos_table, real_part), direction * apply_fn(sin_table, real_part))
    if apply_fn is apply_cols:
        block = jnp.concatenate(
            [
                jnp.concatenate([cos_table, direction * sin_table], axis=1),
                jnp.concatenate([-direction * sin_table, cos_table], axis=1),
            ],
            axis=0,
        )
        both = apply_cols(block, jnp.concatenate([real_part, imag_part], axis=2))
        out_len = cos_table.shape[1]
        return (both[:, :, :out_len], both[:, :, out_len:])
    block = jnp.concatenate(
        [
            jnp.concatenate([cos_table, -direction * sin_table], axis=1),
            jnp.concatenate([direction * sin_table, cos_table], axis=1),
        ],
        axis=0,
    )
    both = apply_rows(block, jnp.concatenate([real_part, imag_part], axis=1))
    out_len = cos_table.shape[0]
    return (both[:, :out_len], both[:, out_len:])


def rotate(real_part, imag_part, tables, direction):
    cos_table, sin_table = tables
    new_real = real_part * cos_table - direction * imag_part * sin_table
    new_imag = direction * real_part * sin_table + imag_part * cos_table
    return (new_real, new_imag)


def forward_local(real_part, imag_part, first_len, ctx_count, ctx_index):
    rows_real = real_part.shape[1]
    padded_len = first_len * ctx_count * ctx_count
    first_tables = grid_product(first_len, rows_real, first_len)
    real_part, imag_part = dft_section(apply_rows, real_part, imag_part, first_tables, -1.0)
    real_part, imag_part = rotate(
        real_part, imag_part, grid_product(first_len, ctx_count, first_len * ctx_count), -1.0
    )
    cos_table, sin_table = grid_product(ctx_count, ctx_count, ctx_count)
    block = jnp.concatenate(
        [
            jnp.concatenate([cos_table, -sin_table], axis=1),
            jnp.concatenate([sin_table, cos_table], axis=1),
        ],
        axis=0,
    )
    both = jnp.einsum(
        "ckn,nm->mck", jnp.concatenate([real_part, imag_part], axis=2), block,
        precision=HIGHEST,
    )
    freq_second = lax.broadcasted_iota(jnp.int32, (ctx_count, 1, first_len), 0)
    freq_first = lax.broadcasted_iota(jnp.int32, (ctx_count, 1, first_len), 2)
    twist = trig_pair((freq_first + first_len * freq_second) * ctx_index, padded_len)
    real_part, imag_part = rotate(both[:ctx_count], both[ctx_count:], twist, -1.0)
    return jnp.stack([real_part, imag_part], axis=1).reshape(ctx_count, -1)


def causal_three(values, before, taps):
    extended = jnp.concatenate([before.astype(jnp.float32), values.astype(jnp.float32)], axis=1)
    return (
        taps[:, 0:1] * extended[:, 2:]
        + taps[:, 1:2] * extended[:, 1:-1]
        + taps[:, 2:3] * extended[:, :-2]
    )


def shards(query_proj, key_proj, value_proj, short_taps, long_filter, skip_scale, norm_gain):
    chan_count = query_proj.shape[0]
    tok_count = query_proj.shape[1]
    ctx_count = lax.axis_size("ctx")
    ctx_index = lax.axis_index("ctx")
    row_count = tok_count // ctx_count
    first_len = 2 * row_count
    padded_len = first_len * ctx_count * ctx_count
    filter_count = long_filter.shape[0]
    pair_count = chan_count // 2
    tails = jnp.stack([query_proj[:, -2:], key_proj[:, -2:], value_proj[:, -2:]])
    before = shifted(tails, "ctx", 1)
    q_conv = causal_three(query_proj, before[0], short_taps[0])
    k_conv = causal_three(key_proj, before[1], short_taps[1])
    v_conv = causal_three(value_proj, before[2], short_taps[2])
    product = k_conv * v_conv
    halves = product.reshape(filter_count, 2, -1, tok_count)
    both_in = jnp.concatenate(
        [
            halves[:, 0].reshape(pair_count, tok_count),
            long_filter,
            halves[:, 1].reshape(pair_count, tok_count),
            jnp.zeros_like(long_filter),
        ],
        axis=0,
    )
    row_total = pair_count + filter_count
    moved = lax.all_to_all(
        both_in.reshape(2 * row_total, row_count, ctx_count), "ctx", split_axis=2, concat_axis=1,
        tiled=True,
    )
    moved = moved.reshape(2 * row_total, row_count, ctx_count)
    spec = forward_local(moved[:row_total], moved[row_total:], first_len, ctx_count, ctx_index)
    spec = lax.all_to_all(spec, "ctx", split_axis=0, concat_axis=0, tiled=True)
    spec = spec.reshape(ctx_count, 2 * row_total, first_len).transpose(1, 2, 0)
    square_tables = grid_product(ctx_count, ctx_count, ctx_count)
    spec_real, spec_imag = dft_section(
        apply_cols, spec[:row_total], spec[row_total:], square_tables, -1.0
    )
    data_real = spec_real[:pair_count]
    data_imag = spec_imag[:pair_count]
    filt_real = spec_real[pair_count:]
    filt_imag = spec_imag[pair_count:]
    grouped_shape = (filter_count, pair_count // filter_count, first_len, ctx_count)
    group_real = data_real.reshape(grouped_shape)
    group_imag = data_imag.reshape(grouped_shape)
    prod_real = (group_real * filt_real[:, None] - group_imag * filt_imag[:, None]).reshape(
        data_real.shape
    )
    prod_imag = (group_real * filt_imag[:, None] + group_imag * filt_real[:, None]).reshape(
        data_real.shape
    )
    inv_cos, inv_sin = square_tables
    inv_block = jnp.concatenate(
        [
            jnp.concatenate([inv_cos, inv_sin], axis=1),
            jnp.concatenate([-inv_sin, inv_cos], axis=1),
        ],
        axis=0,
    )
    back = jnp.einsum(
        "ckn,nm->mck", jnp.concatenate([prod_real, prod_imag], axis=2), inv_block,
        precision=HIGHEST,
    )
    time_third = lax.broadcasted_iota(jnp.int32, (ctx_count, 1, first_len), 0)
    freq_first = lax.broadcasted_iota(jnp.int32, (ctx_count, 1, first_len), 2)
    twist = trig_pair((freq_first + first_len * ctx_index) * time_third, padded_len)
    back_real, back_imag = rotate(back[:ctx_count], back[ctx_count:], twist, 1.0)
    back = jnp.stack([back_real, back_imag], axis=1).reshape(ctx_count, -1)
    back = lax.all_to_all(back, "ctx", split_axis=0, concat_axis=0, tiled=True)
    back = back.reshape(ctx_count, 2 * pair_count, first_len).transpose(1, 2, 0)
    back_real, back_imag = dft_section(
        apply_cols, back[:pair_count], back[pair_count:], square_tables, 1.0
    )
    back_real, back_imag = rotate(
        back_real, back_imag, grid_product(first_len, ctx_count, first_len * ctx_count), 1.0
    )
    last_cos, last_sin = grid_product(row_count, first_len, first_len)
    last_block = jnp.concatenate(
        [
            jnp.concatenate([last_cos, -last_sin], axis=1),
            jnp.concatenate([last_sin, last_cos], axis=1),
        ],
        axis=0,
    ) * (1.0 / padded_len)
    time_vals = jnp.einsum(
        "ut,ctq->uqc", last_block, jnp.concatenate([back_real, back_imag], axis=1),
        precision=HIGHEST,
    )
    time_vals = time_vals.reshape(2, row_count, ctx_count, pair_count).transpose(1, 2, 0, 3)
    time_vals = time_vals.reshape(ctx_count, tok_count // ctx_count, chan_count)
    convolved = lax.all_to_all(time_vals, "ctx", split_axis=0, concat_axis=0, tiled=True)
    convolved = convolved.transpose(2, 1, 0).reshape(2, filter_count, -1, tok_count)
    convolved = convolved.transpose(1, 0, 2, 3).reshape(chan_count, tok_count)
    mixed = q_conv * (convolved + skip_scale[:, None] * product)
    power = lax.psum(jnp.sum(mixed * mixed, axis=0), "tp")
    total_channels = chan_count * lax.axis_size("tp")
    return (norm_gain[:, None] * mixed * lax.rsqrt(power / total_channels + 1e-05)).astype(
        jnp.bfloat16
    )


def solution(mesh):
    return jax.shard_map(
        shards,
        mesh=mesh,
        in_specs=(
            P("tp", "ctx"),
            P("tp", "ctx"),
            P("tp", "ctx"),
            P(None, "tp", None),
            P("tp", "ctx"),
            P("tp"),
            P("tp"),
        ),
        out_specs=P("tp", "ctx"),
        check_vma=False,
    )
```

```python
import math

import jax
import jax.numpy as jnp
from jax import lax
from jax.sharding import PartitionSpec as P

HIGHEST = lax.Precision.HIGHEST


def shifted(x, axis, by):
    length = lax.axis_size(axis)
    pairs = [(i, i + by) for i in range(length) if 0 <= i + by < length]
    return lax.ppermute(x, axis, pairs)


def trig_pair(steps_int, modulus):
    angle = (steps_int % modulus).astype(jnp.float32) * (2.0 * math.pi / modulus)
    return (jnp.cos(angle), jnp.sin(angle))


def grid_product(first_len, second_len, modulus):
    left = lax.broadcasted_iota(jnp.int32, (first_len, second_len), 0)
    right = lax.broadcasted_iota(jnp.int32, (first_len, second_len), 1)
    return trig_pair(left * right, modulus)


def apply_rows(table, values):
    return jnp.einsum("kt,ctn->ckn", table, values, precision=HIGHEST)


def apply_cols(table, values):
    return jnp.einsum("ckn,nm->ckm", values, table, precision=HIGHEST)


def dft_section(apply_fn, real_part, imag_part, tables, direction):
    cos_table, sin_table = tables
    if imag_part is None:
        return (apply_fn(cos_table, real_part), direction * apply_fn(sin_table, real_part))
    if apply_fn is apply_cols:
        block = jnp.concatenate(
            [
                jnp.concatenate([cos_table, direction * sin_table], axis=1),
                jnp.concatenate([-direction * sin_table, cos_table], axis=1),
            ],
            axis=0,
        )
        both = apply_cols(block, jnp.concatenate([real_part, imag_part], axis=2))
        out_len = cos_table.shape[1]
        return (both[:, :, :out_len], both[:, :, out_len:])
    block = jnp.concatenate(
        [
            jnp.concatenate([cos_table, -direction * sin_table], axis=1),
            jnp.concatenate([direction * sin_table, cos_table], axis=1),
        ],
        axis=0,
    )
    both = apply_rows(block, jnp.concatenate([real_part, imag_part], axis=1))
    out_len = cos_table.shape[0]
    return (both[:, :out_len], both[:, out_len:])


def rotate(real_part, imag_part, tables, direction):
    cos_table, sin_table = tables
    new_real = real_part * cos_table - direction * imag_part * sin_table
    new_imag = direction * real_part * sin_table + imag_part * cos_table
    return (new_real, new_imag)


def forward_local(real_part, imag_part, first_len, ctx_count, ctx_index):
    rows_real = real_part.shape[1]
    padded_len = first_len * ctx_count * ctx_count
    first_tables = grid_product(first_len, rows_real, first_len)
    real_part, imag_part = dft_section(apply_rows, real_part, imag_part, first_tables, -1.0)
    real_part, imag_part = rotate(
        real_part, imag_part, grid_product(first_len, ctx_count, first_len * ctx_count), -1.0
    )
    cos_table, sin_table = grid_product(ctx_count, ctx_count, ctx_count)
    block = jnp.concatenate(
        [
            jnp.concatenate([cos_table, -sin_table], axis=1),
            jnp.concatenate([sin_table, cos_table], axis=1),
        ],
        axis=0,
    )
    both = jnp.einsum(
        "ckn,nm->mck", jnp.concatenate([real_part, imag_part], axis=2), block,
        precision=HIGHEST,
    )
    freq_second = lax.broadcasted_iota(jnp.int32, (ctx_count, 1, first_len), 0)
    freq_first = lax.broadcasted_iota(jnp.int32, (ctx_count, 1, first_len), 2)
    twist = trig_pair((freq_first + first_len * freq_second) * ctx_index, padded_len)
    real_part, imag_part = rotate(both[:ctx_count], both[ctx_count:], twist, -1.0)
    return jnp.stack([real_part, imag_part], axis=1).reshape(ctx_count, -1)


def causal_three(values, before, taps):
    extended = jnp.concatenate([before.astype(jnp.float32), values.astype(jnp.float32)], axis=1)
    return (
        taps[:, 0:1] * extended[:, 2:]
        + taps[:, 1:2] * extended[:, 1:-1]
        + taps[:, 2:3] * extended[:, :-2]
    )


def shards(query_proj, key_proj, value_proj, short_taps, long_filter, skip_scale, norm_gain):
    chan_count = query_proj.shape[0]
    tok_count = query_proj.shape[1]
    ctx_count = lax.axis_size("ctx")
    ctx_index = lax.axis_index("ctx")
    row_count = tok_count // ctx_count
    first_len = 2 * row_count
    padded_len = first_len * ctx_count * ctx_count
    filter_count = long_filter.shape[0]
    pair_count = chan_count // 2
    tails = jnp.stack([query_proj[:, -2:], key_proj[:, -2:], value_proj[:, -2:]])
    before = shifted(tails, "ctx", 1)
    q_conv = causal_three(query_proj, before[0], short_taps[0])
    k_conv = causal_three(key_proj, before[1], short_taps[1])
    v_conv = causal_three(value_proj, before[2], short_taps[2])
    product = k_conv * v_conv
    halves = product.reshape(filter_count, 2, -1, tok_count)
    both_in = jnp.concatenate(
        [
            halves[:, 0].reshape(pair_count, tok_count),
            long_filter,
            halves[:, 1].reshape(pair_count, tok_count),
            jnp.zeros_like(long_filter),
        ],
        axis=0,
    )
    row_total = pair_count + filter_count
    moved = both_in.reshape(2 * row_total, row_count, ctx_count).transpose(2, 0, 1)
    moved = lax.all_to_all(moved.reshape(ctx_count, -1), "ctx", split_axis=0, concat_axis=0, tiled=True)
    moved = moved.reshape(ctx_count, 2 * row_total, row_count).transpose(1, 0, 2)
    moved = moved.reshape(2 * row_total, row_count, ctx_count)
    spec = forward_local(moved[:row_total], moved[row_total:], first_len, ctx_count, ctx_index)
    spec = lax.all_to_all(spec, "ctx", split_axis=0, concat_axis=0, tiled=True)
    spec = spec.reshape(ctx_count, 2 * row_total, first_len).transpose(1, 2, 0)
    square_tables = grid_product(ctx_count, ctx_count, ctx_count)
    spec_real, spec_imag = dft_section(
        apply_cols, spec[:row_total], spec[row_total:], square_tables, -1.0
    )
    data_real = spec_real[:pair_count]
    data_imag = spec_imag[:pair_count]
    filt_real = spec_real[pair_count:]
    filt_imag = spec_imag[pair_count:]
    grouped_shape = (filter_count, pair_count // filter_count, first_len, ctx_count)
    group_real = data_real.reshape(grouped_shape)
    group_imag = data_imag.reshape(grouped_shape)
    prod_real = (group_real * filt_real[:, None] - group_imag * filt_imag[:, None]).reshape(
        data_real.shape
    )
    prod_imag = (group_real * filt_imag[:, None] + group_imag * filt_real[:, None]).reshape(
        data_real.shape
    )
    inv_cos, inv_sin = square_tables
    inv_block = jnp.concatenate(
        [
            jnp.concatenate([inv_cos, inv_sin], axis=1),
            jnp.concatenate([-inv_sin, inv_cos], axis=1),
        ],
        axis=0,
    )
    back = jnp.einsum(
        "ckn,nm->mck", jnp.concatenate([prod_real, prod_imag], axis=2), inv_block,
        precision=HIGHEST,
    )
    time_third = lax.broadcasted_iota(jnp.int32, (ctx_count, 1, first_len), 0)
    freq_first = lax.broadcasted_iota(jnp.int32, (ctx_count, 1, first_len), 2)
    twist = trig_pair((freq_first + first_len * ctx_index) * time_third, padded_len)
    back_real, back_imag = rotate(back[:ctx_count], back[ctx_count:], twist, 1.0)
    back = jnp.stack([back_real, back_imag], axis=1).reshape(ctx_count, -1)
    back = lax.all_to_all(back, "ctx", split_axis=0, concat_axis=0, tiled=True)
    back = back.reshape(ctx_count, 2 * pair_count, first_len).transpose(1, 2, 0)
    back_real, back_imag = dft_section(
        apply_cols, back[:pair_count], back[pair_count:], square_tables, 1.0
    )
    back_real, back_imag = rotate(
        back_real, back_imag, grid_product(first_len, ctx_count, first_len * ctx_count), 1.0
    )
    last_cos, last_sin = grid_product(row_count, first_len, first_len)
    last_block = jnp.concatenate(
        [
            jnp.concatenate([last_cos, -last_sin], axis=1),
            jnp.concatenate([last_sin, last_cos], axis=1),
        ],
        axis=0,
    ) * (1.0 / padded_len)
    time_vals = jnp.einsum(
        "ut,ctq->uqc", last_block, jnp.concatenate([back_real, back_imag], axis=1),
        precision=HIGHEST,
    )
    time_vals = time_vals.reshape(2, row_count, ctx_count, pair_count).transpose(1, 2, 0, 3)
    time_vals = time_vals.reshape(ctx_count, tok_count // ctx_count, chan_count)
    convolved = lax.all_to_all(time_vals, "ctx", split_axis=0, concat_axis=0, tiled=True)
    convolved = convolved.transpose(2, 1, 0).reshape(2, filter_count, -1, tok_count)
    convolved = convolved.transpose(1, 0, 2, 3).reshape(chan_count, tok_count)
    mixed = q_conv * (convolved + skip_scale[:, None] * product)
    power = lax.psum(jnp.sum(mixed * mixed, axis=0), "tp")
    total_channels = chan_count * lax.axis_size("tp")
    return (norm_gain[:, None] * mixed * lax.rsqrt(power / total_channels + 1e-05)).astype(
        jnp.bfloat16
    )


def solution(mesh):
    return jax.shard_map(
        shards,
        mesh=mesh,
        in_specs=(
            P("tp", "ctx"),
            P("tp", "ctx"),
            P("tp", "ctx"),
            P(None, "tp", None),
            P("tp", "ctx"),
            P("tp"),
            P("tp"),
        ),
        out_specs=P("tp", "ctx"),
        check_vma=False,
    )
```

```python
import math

import jax
import jax.numpy as jnp
from jax import lax
from jax.sharding import PartitionSpec as P

HIGHEST = lax.Precision.HIGHEST


def shifted(x, axis, by):
    length = lax.axis_size(axis)
    pairs = [(i, i + by) for i in range(length) if 0 <= i + by < length]
    return lax.ppermute(x, axis, pairs)


def trig_pair(steps_int, modulus):
    angle = (steps_int % modulus).astype(jnp.float32) * (2.0 * math.pi / modulus)
    return (jnp.cos(angle), jnp.sin(angle))


def grid_product(first_len, second_len, modulus):
    left = lax.broadcasted_iota(jnp.int32, (first_len, second_len), 0)
    right = lax.broadcasted_iota(jnp.int32, (first_len, second_len), 1)
    return trig_pair(left * right, modulus)


def apply_rows(table, values):
    return jnp.einsum("kt,ctn->ckn", table, values, precision=HIGHEST)


def apply_cols(table, values):
    return jnp.einsum("ckn,nm->ckm", values, table, precision=HIGHEST)


def dft_section(apply_fn, real_part, imag_part, tables, direction):
    cos_table, sin_table = tables
    if imag_part is None:
        return (apply_fn(cos_table, real_part), direction * apply_fn(sin_table, real_part))
    if apply_fn is apply_cols:
        block = jnp.concatenate(
            [
                jnp.concatenate([cos_table, direction * sin_table], axis=1),
                jnp.concatenate([-direction * sin_table, cos_table], axis=1),
            ],
            axis=0,
        )
        both = apply_cols(block, jnp.concatenate([real_part, imag_part], axis=2))
        out_len = cos_table.shape[1]
        return (both[:, :, :out_len], both[:, :, out_len:])
    block = jnp.concatenate(
        [
            jnp.concatenate([cos_table, -direction * sin_table], axis=1),
            jnp.concatenate([direction * sin_table, cos_table], axis=1),
        ],
        axis=0,
    )
    both = apply_rows(block, jnp.concatenate([real_part, imag_part], axis=1))
    out_len = cos_table.shape[0]
    return (both[:, :out_len], both[:, out_len:])


def rotate(real_part, imag_part, tables, direction):
    cos_table, sin_table = tables
    new_real = real_part * cos_table - direction * imag_part * sin_table
    new_imag = direction * real_part * sin_table + imag_part * cos_table
    return (new_real, new_imag)


def forward_local(real_part, imag_part, first_len, ctx_count, ctx_index):
    rows_real = real_part.shape[1]
    padded_len = first_len * ctx_count * ctx_count
    first_tables = grid_product(first_len, rows_real, first_len)
    real_part, imag_part = dft_section(apply_rows, real_part, imag_part, first_tables, -1.0)
    real_part, imag_part = rotate(
        real_part, imag_part, grid_product(first_len, ctx_count, first_len * ctx_count), -1.0
    )
    cos_table, sin_table = grid_product(ctx_count, ctx_count, ctx_count)
    block = jnp.concatenate(
        [
            jnp.concatenate([cos_table, -sin_table], axis=1),
            jnp.concatenate([sin_table, cos_table], axis=1),
        ],
        axis=0,
    )
    both = jnp.einsum(
        "ckn,nm->mck", jnp.concatenate([real_part, imag_part], axis=2), block,
        precision=HIGHEST,
    )
    freq_second = lax.broadcasted_iota(jnp.int32, (ctx_count, 1, first_len), 0)
    freq_first = lax.broadcasted_iota(jnp.int32, (ctx_count, 1, first_len), 2)
    twist = trig_pair((freq_first + first_len * freq_second) * ctx_index, padded_len)
    real_part, imag_part = rotate(both[:ctx_count], both[ctx_count:], twist, -1.0)
    return jnp.stack([real_part, imag_part], axis=1).reshape(ctx_count, -1)


def causal_three(values, before, taps):
    extended = jnp.concatenate([before.astype(jnp.float32), values.astype(jnp.float32)], axis=1)
    return (
        taps[:, 0:1] * extended[:, 2:]
        + taps[:, 1:2] * extended[:, 1:-1]
        + taps[:, 2:3] * extended[:, :-2]
    )


def shards(query_proj, key_proj, value_proj, short_taps, long_filter, skip_scale, norm_gain):
    chan_count = query_proj.shape[0]
    tok_count = query_proj.shape[1]
    ctx_count = lax.axis_size("ctx")
    ctx_index = lax.axis_index("ctx")
    row_count = tok_count // ctx_count
    first_len = 2 * row_count
    padded_len = first_len * ctx_count * ctx_count
    filter_count = long_filter.shape[0]
    pair_count = chan_count // 2
    tails = jnp.stack([query_proj[:, -2:], key_proj[:, -2:], value_proj[:, -2:]])
    before = shifted(tails, "ctx", 1)
    q_conv = causal_three(query_proj, before[0], short_taps[0])
    k_conv = causal_three(key_proj, before[1], short_taps[1])
    v_conv = causal_three(value_proj, before[2], short_taps[2])
    product = k_conv * v_conv
    halves = product.reshape(filter_count, 2, -1, tok_count)
    both_in = jnp.concatenate(
        [
            halves[:, 0].reshape(pair_count, tok_count),
            long_filter,
            halves[:, 1].reshape(pair_count, tok_count),
            jnp.zeros_like(long_filter),
        ],
        axis=0,
    )
    row_total = pair_count + filter_count
    moved = both_in.reshape(2 * row_total, row_count, ctx_count).transpose(2, 0, 1)
    moved = lax.all_to_all(moved.reshape(ctx_count, -1), "ctx", split_axis=0, concat_axis=0, tiled=True)
    moved = moved.reshape(ctx_count, 2 * row_total, row_count).transpose(1, 0, 2)
    moved = moved.reshape(2 * row_total, row_count, ctx_count)
    spec = forward_local(moved[:row_total], moved[row_total:], first_len, ctx_count, ctx_index)
    spec = lax.all_to_all(spec, "ctx", split_axis=0, concat_axis=0, tiled=True)
    square_tables = grid_product(ctx_count, ctx_count, ctx_count)
    fwd_cos, fwd_sin = square_tables
    gather_block = jnp.stack(
        [jnp.stack([fwd_cos, -fwd_sin], axis=1), jnp.stack([fwd_sin, fwd_cos], axis=1)], axis=1
    )
    spec = jnp.einsum(
        "jhrk,jhum->urkm", spec.reshape(ctx_count, 2, row_total, first_len), gather_block,
        precision=HIGHEST,
    )
    spec_real, spec_imag = spec[0], spec[1]
    data_real = spec_real[:pair_count]
    data_imag = spec_imag[:pair_count]
    filt_real = spec_real[pair_count:]
    filt_imag = spec_imag[pair_count:]
    grouped_shape = (filter_count, pair_count // filter_count, first_len, ctx_count)
    group_real = data_real.reshape(grouped_shape)
    group_imag = data_imag.reshape(grouped_shape)
    prod_real = (group_real * filt_real[:, None] - group_imag * filt_imag[:, None]).reshape(
        data_real.shape
    )
    prod_imag = (group_real * filt_imag[:, None] + group_imag * filt_real[:, None]).reshape(
        data_real.shape
    )
    inv_cos, inv_sin = square_tables
    inv_block = jnp.concatenate(
        [
            jnp.concatenate([inv_cos, inv_sin], axis=1),
            jnp.concatenate([-inv_sin, inv_cos], axis=1),
        ],
        axis=0,
    )
    back = jnp.einsum(
        "ckn,nm->mck", jnp.concatenate([prod_real, prod_imag], axis=2), inv_block,
        precision=HIGHEST,
    )
    time_third = lax.broadcasted_iota(jnp.int32, (ctx_count, 1, first_len), 0)
    freq_first = lax.broadcasted_iota(jnp.int32, (ctx_count, 1, first_len), 2)
    twist = trig_pair((freq_first + first_len * ctx_index) * time_third, padded_len)
    back_real, back_imag = rotate(back[:ctx_count], back[ctx_count:], twist, 1.0)
    back = jnp.stack([back_real, back_imag], axis=1).reshape(ctx_count, -1)
    back = lax.all_to_all(back, "ctx", split_axis=0, concat_axis=0, tiled=True)
    back = back.reshape(ctx_count, 2 * pair_count, first_len).transpose(1, 2, 0)
    back_real, back_imag = dft_section(
        apply_cols, back[:pair_count], back[pair_count:], square_tables, 1.0
    )
    back_real, back_imag = rotate(
        back_real, back_imag, grid_product(first_len, ctx_count, first_len * ctx_count), 1.0
    )
    last_cos, last_sin = grid_product(row_count, first_len, first_len)
    last_block = jnp.concatenate(
        [
            jnp.concatenate([last_cos, -last_sin], axis=1),
            jnp.concatenate([last_sin, last_cos], axis=1),
        ],
        axis=0,
    ) * (1.0 / padded_len)
    time_vals = jnp.einsum(
        "ut,ctq->uqc", last_block, jnp.concatenate([back_real, back_imag], axis=1),
        precision=HIGHEST,
    )
    time_vals = time_vals.reshape(2, row_count, ctx_count, pair_count).transpose(1, 2, 0, 3)
    time_vals = time_vals.reshape(ctx_count, tok_count // ctx_count, chan_count)
    convolved = lax.all_to_all(time_vals, "ctx", split_axis=0, concat_axis=0, tiled=True)
    convolved = convolved.transpose(2, 1, 0).reshape(2, filter_count, -1, tok_count)
    convolved = convolved.transpose(1, 0, 2, 3).reshape(chan_count, tok_count)
    mixed = q_conv * (convolved + skip_scale[:, None] * product)
    power = lax.psum(jnp.sum(mixed * mixed, axis=0), "tp")
    total_channels = chan_count * lax.axis_size("tp")
    return (norm_gain[:, None] * mixed * lax.rsqrt(power / total_channels + 1e-05)).astype(
        jnp.bfloat16
    )


def solution(mesh):
    return jax.shard_map(
        shards,
        mesh=mesh,
        in_specs=(
            P("tp", "ctx"),
            P("tp", "ctx"),
            P("tp", "ctx"),
            P(None, "tp", None),
            P("tp", "ctx"),
            P("tp"),
            P("tp"),
        ),
        out_specs=P("tp", "ctx"),
        check_vma=False,
    )
```
